512 devices in a mesh: vox: 128 (over z, y, core), ch: 4 (over x).
Axes of the slice: x: 4, y: 4, z: 16, core: 2. Of those that a mesh axis runs over, the one named last changes fastest.
Arguments:
- features: bfloat16 [131072, 128], P('vox'), may hold values from -6 to 6
- kernel: bfloat16 [27, 256, 128], P(None, 'ch'), may hold values from -0.1875 to 0.1875
- coarse_grad: bfloat16 [256, 65536], P('ch', 'vox'), may hold values from -6 to 6
- pair_fine: int32 [524288], P('vox'), may hold values from 0 to 1023
- pair_target: int32 [524288], P('vox'), may hold values from 0 to 511
- block_offset: int32 [4096], P('vox'), may hold values from 0 to 26
- target_owner: int32 [65536, 1], P('vox'), may hold values from 0 to 127; in each aligned block of 512 rows (0 to 511, 512 to 1023, ...) at most 6 rows name the same one
- slot_coarse_row: int32 [98304], P('vox'), may hold values from 0 to 511
- fine_count: int32 [128], P('vox'), may hold values from 512 to 1024, as said below
Outputs:
- activation: bfloat16 [256, 65536], P('ch', 'vox')
- grad_features: bfloat16 [128, 131072], P('ch', 'vox')
- grad_kernel: bfloat16 [27, 256, 128], P(None, 'ch')
The draws below stay inside these ranges and needn't reach their ends.
Inputs may be any that keep to these rules, and one draw needn't show every extreme that they name: `target_owner`: among the 512 targets of one block no owner appears more than 6 times, and in some block one owner appears exactly 6 times. `fine_count`: some block has all 1024 fine voxels live.
All inputs are finite; a program needn't handle non-finite values.
Results may differ from the reference program's by a relative error of at most 0.0053.
Values may be sent and summed in bfloat16 or wider, within the bound.
No kernel may reach another device: no remote copies, remote signals or barrier semaphores. Data moves between devices by JAX's collectives and lax.ppermute only.
A program may use at most 64 MiB of HBM per device.

```python
import math
import jax
import jax.numpy as jnp
import numpy as np
from jax import lax

CF = 128
CC = 256
KOFF = 27
FR = 1024
PAIRS = 4096
TG = 512
COARSE_PER_VOXEL = 512
OWNERS = 128
SLOT = 6
NF = 131072
NC = 65536
NPAIRS = 524288
NBLOCKS = 4096
TARGETS = 65536
RECEIVE_SLOTS = 98304


def draw_fine_count(key, part):
    first_key, second_key = jax.random.split(jax.random.fold_in(key, 11))
    counts = jax.random.randint(first_key, (OWNERS,), FR // 2, FR + 1)
    chosen = jax.random.randint(second_key, (), 0, OWNERS)
    return jnp.where(jnp.arange(OWNERS) == chosen, FR, counts).astype(jnp.int32)


def place_ends(array, own_key, least, largest):
    dims = array.shape
    place = [jax.random.randint(jax.random.fold_in(own_key, axis), (), 0, dims[axis]) for axis in range(len(dims))]
    array = array.at[tuple(place)].set(least)
    longest = dims.index(max(dims))
    place[longest] = (place[longest] + 1) % dims[longest]
    return array.at[tuple(place)].set(largest)


def shard_levels(rng, dims, cuts, low, largest):
    def one(position, shards_of):
        heights = jax.random.uniform(jax.random.fold_in(jax.random.fold_in(rng, 6), position), (shards_of,), jnp.float32, low / len(cuts), largest / len(cuts))
        return jnp.repeat(jnp.exp(heights), dims[position] // shards_of).reshape((-1,) + (1,) * (len(dims) - position - 1))

    factor_of = one(*cuts[0])
    for cut in cuts[1:]:
        factor_of = factor_of * one(*cut)
    return factor_of


def routed_block(key, own, number, rows, number_of, top, reach, lean):
    order = jax.random.permutation(key, number_of)
    crowded, ordinary = load_shares(number_of, rows * top, reach, lean, True), load_shares(number_of, rows * top, reach, lean, False)
    places = jnp.arange(number_of)

    def named(tallies, turn):
        used = int((tallies > 0).sum())
        fixed = max(1, used // 4)
        shifted = fixed + (places - fixed + turn * (used - fixed)) % max(1, number_of - fixed)
        return jnp.zeros((number_of,), jnp.int32).at[order[jnp.where(places < fixed, places, shifted)]].set(jnp.asarray(tallies, jnp.int32))

    tallies = jnp.where(number % 4 == 0, named(crowded, number // 4), named(ordinary, number - number // 4 - 1))
    mixed = jax.random.permutation(jax.random.fold_in(own, 3), number_of)
    source_of, taker = mixed[0:number_of // 2 * 2:2], mixed[1:number_of // 2 * 2:2]
    room = jnp.minimum(tallies[source_of] - 1, reach - tallies[taker]) // 2
    room = jnp.where((source_of == order[0]) | (taker == order[0]) | (tallies[taker] == 0), 0, jnp.maximum(room, 0))
    shifted = jax.random.randint(jax.random.fold_in(own, 4), (number_of // 2,), 0, 1 << 20) % (room + 1)
    tallies = tallies.at[source_of].add(-shifted).at[taker].add(shifted)
    members = jnp.searchsorted(jnp.cumsum(tallies), jnp.arange(rows * top), side="right").astype(jnp.int32)
    table = members.reshape(top, rows).T
    table = table[jax.random.permutation(jax.random.fold_in(own, 1), rows)]
    turn = jax.random.randint(jax.random.fold_in(own, 2), (rows, 1), 0, top)
    return jnp.take_along_axis(table, (jnp.arange(top)[None, :] + turn) % top, axis=1)


def load_shares(number_of, total, bound, slope, full):
    portions = [(1 << 20) // math.isqrt(standing ** slope) + 1 for standing in range(1, number_of + 1)]
    largest = bound if full else min(bound, max(-(-total // number_of), total * portions[0] // sum(portions)))
    least = 1 if total - largest >= number_of - 1 else 0
    given, spare = [largest] + [least] * (number_of - 1), total - largest - least * (number_of - 1)
    while spare > 0:
        candidates = [i for i in range(1, number_of) if given[i] < largest] or [i for i in range(1, number_of) if given[i] < bound]
        pool, left = sum([portions[i] for i in candidates]), spare
        for i in candidates:
            addition = min(bound - given[i], max(1, left * portions[i] // pool), spare)
            given[i] = given[i] + addition
            spare = spare - addition
    return np.array(given)


def gaussian(own_key, shape, width, limit, cuts=(), kind=jnp.bfloat16):
    values = width * jax.random.normal(own_key, shape, jnp.float32)
    if cuts:
        values = values * shard_levels(own_key, shape, cuts, -0.22, 0.18)
    return jnp.clip(values, -limit, limit).astype(kind)


def setup_inputs(seed: int = 0) -> dict:
    arg_keys = jax.random.split(jax.random.key(seed), 10)
    features = gaussian(arg_keys[0], (NF, CF), 1.0, 6.0, ((0, 128),))
    kernel = gaussian(arg_keys[1], (KOFF, CC, CF), (8 * CF) ** -0.5, 0.1875, ((1, 4),))
    coarse_grad = gaussian(arg_keys[2], (CC, NC), 1.0, 6.0, ((0, 4), (1, 128)))
    pair_fine = place_ends(jax.random.randint(arg_keys[3], (NPAIRS,), 0, FR), jax.random.fold_in(arg_keys[3], 1), 0, FR - 1).astype(jnp.int32)
    pair_target = place_ends(jax.random.randint(arg_keys[4], (NPAIRS,), 0, TG), jax.random.fold_in(arg_keys[4], 1), 0, TG - 1).astype(jnp.int32)
    block_offset = place_ends(jax.random.randint(arg_keys[5], (NBLOCKS,), 0, KOFF), jax.random.fold_in(arg_keys[5], 1), 0, KOFF - 1).astype(jnp.int32)
    target_owner_keys = jax.random.split(jax.random.fold_in(arg_keys[6], 1), TARGETS // TG)
    target_owner_turns = jax.random.permutation(jax.random.fold_in(arg_keys[6], 3), TARGETS // TG)
    target_owner = jax.vmap(lambda own, number: routed_block(jax.random.fold_in(arg_keys[6], 2), own, number, TG, OWNERS, 1, SLOT, 2))(target_owner_keys, target_owner_turns).reshape((TARGETS, 1))
    slot_coarse_row = place_ends(jax.random.randint(arg_keys[7], (RECEIVE_SLOTS,), 0, COARSE_PER_VOXEL), jax.random.fold_in(arg_keys[7], 1), 0, COARSE_PER_VOXEL - 1).astype(jnp.int32)
    fine_count = draw_fine_count(jax.random.fold_in(arg_keys[9], 71), 0)
    return dict(features=features, kernel=kernel, coarse_grad=coarse_grad, pair_fine=pair_fine, pair_target=pair_target, block_offset=block_offset, target_owner=target_owner, slot_coarse_row=slot_coarse_row, fine_count=fine_count)


def owner_slots(owner_of):
    labels = jnp.arange(OWNERS, dtype=jnp.int32)
    onehot = (owner_of[:, None] == labels[None, :]).astype(jnp.int32)
    before = jnp.cumsum(onehot, axis=0) - onehot
    return lax.optimization_barrier(jnp.sum(before * onehot, axis=1)).astype(jnp.int32)

def reference(features, kernel, coarse_grad, pair_fine, pair_target, block_offset, target_owner, slot_coarse_row, fine_count):
    blocks = PAIRS // 128
    live_mask = jnp.arange(FR, dtype=jnp.int32)[None, :] < fine_count[:, None]
    fine = jnp.where(live_mask[:, :, None], features.reshape(OWNERS, FR, CF), jnp.zeros((), features.dtype))
    fine_ids = pair_fine.reshape(OWNERS, PAIRS)
    target_ids = pair_target.reshape(OWNERS, PAIRS)
    offset_ids = block_offset.reshape(OWNERS, blocks)
    owner_of = target_owner.reshape(OWNERS, TG)
    kernel_weight = jnp.transpose(kernel.astype(jnp.float32), (0, 2, 1))

    def forward_one(pieces):
        fine_dev, fine_at, target_at, offset_at = pieces
        gathered = fine_dev[fine_at].astype(jnp.float32).reshape(blocks, 128, CF)
        partial_value = jnp.einsum('bpc,bco->bpo', gathered, kernel_weight[offset_at]).reshape(PAIRS, CC)
        return jax.ops.segment_sum(partial_value, target_at, TG).astype(jnp.bfloat16)
    target_part = lax.map(forward_one, (fine, fine_ids, target_ids, offset_ids))
    slot_of = lax.map(owner_slots, owner_of)
    source = jnp.arange(OWNERS, dtype=jnp.int32)[:, None]
    place_at = owner_of * (OWNERS * SLOT) + source * SLOT + slot_of
    destination = (owner_of * COARSE_PER_VOXEL + slot_coarse_row[place_at]).astype(jnp.int32)
    coarse = jax.ops.segment_sum(target_part.reshape(OWNERS * TG, CC).astype(jnp.float32), destination.reshape(-1), NC)
    gate_output = jax.nn.sigmoid(coarse)
    activation = (coarse * gate_output).astype(jnp.bfloat16)
    grad_coarse = (coarse_grad.astype(jnp.float32).T * gate_output * (1.0 + coarse * (1.0 - gate_output))).astype(jnp.bfloat16)

    def backward_one(reduced_total, pieces):
        fine_dev, fine_at, target_at, offset_at, dest_dev, live_dev = pieces
        gathered = fine_dev[fine_at].astype(jnp.float32).reshape(blocks, 128, CF)
        grad_rows = grad_coarse[dest_dev][target_at].astype(jnp.float32).reshape(blocks, 128, CC)
        grad_in = jnp.einsum('bpo,bco->bpc', grad_rows, kernel_weight[offset_at]).reshape(PAIRS, CF)
        fine_sum = jax.ops.segment_sum(grad_in, fine_at, FR)
        fine_grad = jnp.where(live_dev[:, None], fine_sum, jnp.zeros((), fine_sum.dtype)).astype(jnp.bfloat16)
        grad_weight = jnp.einsum('bpc,bpo->boc', gathered, grad_rows)
        reduced_total = reduced_total + jax.ops.segment_sum(grad_weight, offset_at, KOFF)
        return (reduced_total, fine_grad)
    reduced_total, fine_grads = lax.scan(backward_one, jnp.zeros((KOFF, CC, CF), jnp.float32), (fine, fine_ids, target_ids, offset_ids, destination, live_mask))
    factor = math.sqrt(KOFF / NPAIRS)
    grad_kernel = (reduced_total * factor).astype(jnp.bfloat16)
    return (activation.T, fine_grads.reshape(NF, CF).T, grad_kernel)
```

```python
import math

import jax
import jax.numpy as jnp
from jax import lax
from jax.sharding import PartitionSpec as P


def owner_slots(owner_of, owners):
    labels = jnp.arange(owners, dtype=jnp.int32)
    onehot = (owner_of[:, None] == labels[None, :]).astype(jnp.int32)
    before = jnp.cumsum(onehot, axis=0) - onehot
    return jnp.sum(before * onehot, axis=1)


def reduce_replicate(weight_sum, owners, factor):
    shape = weight_sum.shape
    rows = weight_sum.size // 128
    chunk = -(-rows // owners)
    flat = jnp.pad(weight_sum.reshape(rows, 128), ((0, chunk * owners - rows), (0, 0)))
    got = lax.all_to_all(flat, "vox", 0, 0, tiled=True)
    mine = (got.reshape(owners, chunk, 128).sum(axis=0) * factor).astype(jnp.bfloat16)
    spread = jnp.broadcast_to(mine[None], (owners, chunk, 128)).reshape(owners * chunk, 128)
    back = lax.all_to_all(spread, "vox", 0, 0, tiled=True)
    return back[:rows].reshape(shape)


def body(
    features,
    kernel,
    coarse_grad,
    pair_fine,
    pair_target,
    block_offset,
    target_owner,
    slot_coarse_row,
    fine_count,
):
    owners = lax.axis_size("vox")
    fine_total, width_in = features.shape
    width_out, coarse_total = coarse_grad.shape
    offsets_all = kernel.shape[0]
    targets = target_owner.shape[0]
    capacity = slot_coarse_row.shape[0] // owners
    blocks = block_offset.shape[0]
    rows_each_turn = min(16, blocks)
    rounds = blocks // rows_each_turn
    live_mask = jnp.arange(fine_total, dtype=jnp.int32) < fine_count[0]
    masked = jnp.where(live_mask[:, None], features, jnp.zeros((), features.dtype))
    fine_ids = pair_fine.reshape(rounds, rows_each_turn, 128)
    target_ids = pair_target.reshape(rounds, rows_each_turn, 128)
    offset_ids = block_offset.reshape(rounds, rows_each_turn)

    def forward_step(totals, pieces):
        fine_at, target_at, offset_at = pieces
        gathered = masked[fine_at]
        partial_value = jnp.einsum(
            "gpc,goc->gpo", gathered, kernel[offset_at], preferred_element_type=jnp.float32
        )
        return (totals.at[target_at.reshape(-1)].add(partial_value.reshape(-1, width_out)), None)

    target_sum, leftover = lax.scan(
        forward_step,
        jnp.zeros((targets, width_out), jnp.float32),
        (fine_ids, target_ids, offset_ids),
    )
    target_part = target_sum.astype(jnp.bfloat16)
    owner_of = target_owner[:, 0]
    slot_index = owner_of * capacity + owner_slots(owner_of, owners)
    send_rows = (
        jnp.zeros((owners * capacity, width_out), jnp.bfloat16).at[slot_index].set(target_part)
    )
    as_lanes = capacity * width_out % 128 == 0
    lane_shape = (owners * capacity * width_out // 128, 128)
    received = lax.all_to_all(
        send_rows.reshape(lane_shape), "vox", split_axis=0, concat_axis=0, tiled=True
    )
    got_rows = received.reshape(owners * capacity, width_out).astype(jnp.float32)
    coarse = jax.ops.segment_sum(got_rows, slot_coarse_row, coarse_total)
    gate_output = jax.nn.sigmoid(coarse)
    activation = (coarse * gate_output).astype(jnp.bfloat16)
    grad_coarse = (
        coarse_grad.astype(jnp.float32).T * gate_output * (1.0 + coarse * (1.0 - gate_output))
    ).astype(jnp.bfloat16)
    back_rows = grad_coarse[slot_coarse_row]
    returned = lax.all_to_all(
        back_rows.reshape(lane_shape), "vox", split_axis=0, concat_axis=0, tiled=True
    )
    grad_target = returned.reshape(owners * capacity, width_out)[slot_index]
    weight_init = jnp.zeros((offsets_all, width_out, width_in), jnp.float32)

    def reverse_update(state_pair, pieces):
        fine_sum, weight_sum = state_pair
        fine_at, target_at, offset_at = pieces
        gathered = masked[fine_at]
        grad_rows = grad_target[target_at]
        grad_in = jnp.einsum(
            "gpo,goc->gpc", grad_rows, kernel[offset_at], preferred_element_type=jnp.float32
        )
        fine_sum = fine_sum.at[fine_at.reshape(-1)].add(grad_in.reshape(-1, width_in))
        grad_weight = jnp.einsum(
            "gpc,gpo->goc", gathered, grad_rows, preferred_element_type=jnp.float32
        )
        return ((fine_sum, weight_sum.at[offset_at].add(grad_weight)), None)

    (fine_sum, weight_sum), leftover = lax.scan(
        reverse_update,
        (jnp.zeros((fine_total, width_in), jnp.float32), weight_init),
        (fine_ids, target_ids, offset_ids),
    )
    fine_grad = lax.psum_scatter(fine_sum, "ch", scatter_dimension=1, tiled=True)
    grad_features = jnp.where(live_mask[:, None], fine_grad, jnp.zeros((), jnp.float32)).astype(
        jnp.bfloat16
    )
    factor = math.sqrt(offsets_all / (blocks * 128 * owners))
    grad_kernel = reduce_replicate(weight_sum, owners, factor)
    return (activation.T, grad_features.T, grad_kernel)


def solution(mesh):
    in_specs = (
        P("vox", None),
        P(None, "ch", None),
        P("ch", "vox"),
        P("vox"),
        P("vox"),
        P("vox"),
        P("vox", None),
        P("vox"),
        P("vox"),
    )
    out_specs = (P("ch", "vox"), P("ch", "vox"), P(None, "ch", None))
    return jax.shard_map(body, mesh=mesh, in_specs=in_specs, out_specs=out_specs, check_vma=False)
```

```python
import math

import jax
import jax.numpy as jnp
from jax import lax
from jax.sharding import PartitionSpec as P


def owner_slots(owner_of, owners):
    labels = jnp.arange(owners, dtype=jnp.int32)
    onehot = (owner_of[:, None] == labels[None, :]).astype(jnp.int32)
    before = jnp.cumsum(onehot, axis=0) - onehot
    return jnp.sum(before * onehot, axis=1)


def one_hot(index, size):
    return (index[:, None] == jnp.arange(size, dtype=jnp.int32)[None, :]).astype(jnp.bfloat16)


def exact_sum(onehot, values):
    high = values.astype(jnp.bfloat16)
    low = (values - high.astype(jnp.float32)).astype(jnp.bfloat16)
    both = jnp.concatenate([high, low], axis=1)
    total = jnp.einsum("pt,pc->tc", onehot, both, preferred_element_type=jnp.float32)
    width = values.shape[1]
    return total[:, :width] + total[:, width:]


def reduce_replicate(weight_sum, owners, factor):
    shape = weight_sum.shape
    rows = weight_sum.size // 128
    chunk = -(-rows // owners)
    flat = jnp.pad(weight_sum.reshape(rows, 128), ((0, chunk * owners - rows), (0, 0)))
    got = lax.all_to_all(flat, "vox", 0, 0, tiled=True)
    mine = (got.reshape(owners, chunk, 128).sum(axis=0) * factor).astype(jnp.bfloat16)
    spread = jnp.broadcast_to(mine[None], (owners, chunk, 128)).reshape(owners * chunk, 128)
    back = lax.all_to_all(spread, "vox", 0, 0, tiled=True)
    return back[:rows].reshape(shape)


def body(
    features,
    kernel,
    coarse_grad,
    pair_fine,
    pair_target,
    block_offset,
    target_owner,
    slot_coarse_row,
    fine_count,
):
    owners = lax.axis_size("vox")
    fine_total, width_in = features.shape
    width_out, coarse_total = coarse_grad.shape
    offsets_all = kernel.shape[0]
    targets = target_owner.shape[0]
    capacity = slot_coarse_row.shape[0] // owners
    slots = owners * capacity
    blocks = block_offset.shape[0]
    pairs = pair_fine.shape[0]
    group = pairs // blocks
    live_mask = jnp.arange(fine_total, dtype=jnp.int32) < fine_count[0]
    masked = jnp.where(live_mask[:, None], features, jnp.zeros((), features.dtype))
    fine_hot = one_hot(pair_fine, fine_total)
    target_hot = one_hot(pair_target, targets)
    gathered = jnp.dot(fine_hot, masked, preferred_element_type=jnp.float32).astype(jnp.bfloat16)
    gathered = gathered.reshape(blocks, group, width_in)
    weights = kernel[block_offset]
    partial_value = jnp.einsum(
        "bpc,boc->bpo", gathered, weights, preferred_element_type=jnp.float32
    ).reshape(pairs, width_out)
    target_part = exact_sum(target_hot, partial_value).astype(jnp.bfloat16)

    owner_of = target_owner[:, 0]
    slot_index = owner_of * capacity + owner_slots(owner_of, owners)
    slot_hot = one_hot(slot_index, slots)
    send_rows = jnp.einsum(
        "ts,to->so", slot_hot, target_part, preferred_element_type=jnp.float32
    ).astype(jnp.bfloat16)
    lane_shape = (slots * width_out // 128, 128)
    received = lax.all_to_all(
        send_rows.reshape(lane_shape), "vox", split_axis=0, concat_axis=0, tiled=True
    )
    got_rows = received.reshape(slots, width_out)
    row_hot = one_hot(slot_coarse_row, coarse_total)
    coarse = jnp.einsum("sc,so->co", row_hot, got_rows, preferred_element_type=jnp.float32)
    gate_output = jax.nn.sigmoid(coarse)
    activation = (coarse * gate_output).astype(jnp.bfloat16)
    grad_coarse = (
        coarse_grad.astype(jnp.float32).T * gate_output * (1.0 + coarse * (1.0 - gate_output))
    ).astype(jnp.bfloat16)
    back_rows = jnp.einsum(
        "sc,co->so", row_hot, grad_coarse, preferred_element_type=jnp.float32
    ).astype(jnp.bfloat16)
    returned = lax.all_to_all(
        back_rows.reshape(lane_shape), "vox", split_axis=0, concat_axis=0, tiled=True
    )
    grad_target = jnp.einsum(
        "ts,so->to", slot_hot, returned.reshape(slots, width_out), preferred_element_type=jnp.float32
    ).astype(jnp.bfloat16)
    grad_rows = jnp.einsum(
        "pt,to->po", target_hot, grad_target, preferred_element_type=jnp.float32
    ).astype(jnp.bfloat16)
    grad_rows = grad_rows.reshape(blocks, group, width_out)
    grad_in = jnp.einsum(
        "bpo,boc->bpc", grad_rows, weights, preferred_element_type=jnp.float32
    ).reshape(pairs, width_in)
    fine_sum = exact_sum(fine_hot, grad_in)
    fine_grad = lax.psum_scatter(fine_sum, "ch", scatter_dimension=1, tiled=True)
    grad_features = jnp.where(live_mask[:, None], fine_grad, jnp.zeros((), jnp.float32)).astype(
        jnp.bfloat16
    )
    grad_weight = jnp.einsum(
        "bpc,bpo->boc", gathered, grad_rows, preferred_element_type=jnp.float32
    )
    weight_sum = (
        jnp.zeros((offsets_all, width_out, width_in), jnp.float32).at[block_offset].add(grad_weight)
    )
    factor = math.sqrt(offsets_all / (blocks * group * owners))
    grad_kernel = reduce_replicate(weight_sum, owners, factor)
    return (activation.T, grad_features.T, grad_kernel)


def solution(mesh):
    in_specs = (
        P("vox", None),
        P(None, "ch", None),
        P("ch", "vox"),
        P("vox"),
        P("vox"),
        P("vox"),
        P("vox", None),
        P("vox"),
        P("vox"),
    )
    out_specs = (P("ch", "vox"), P("ch", "vox"), P(None, "ch", None))
    return jax.shard_map(body, mesh=mesh, in_specs=in_specs, out_specs=out_specs, check_vma=False)
```

```python
import math

import jax
import jax.numpy as jnp
from jax import lax
from jax.sharding import PartitionSpec as P


def owner_slots(owner_of, owners):
    labels = jnp.arange(owners, dtype=jnp.int32)
    onehot = (owner_of[:, None] == labels[None, :]).astype(jnp.int32)
    before = jnp.cumsum(onehot, axis=0) - onehot
    return jnp.sum(before * onehot, axis=1)


def one_hot(index, size):
    return (index[:, None] == jnp.arange(size, dtype=jnp.int32)[None, :]).astype(jnp.bfloat16)


def exact_sum(onehot, values):
    high = lax.reduce_precision(values, exponent_bits=8, mantissa_bits=7)
    low = values - high
    both = jnp.concatenate([high.astype(jnp.bfloat16), low.astype(jnp.bfloat16)], axis=1)
    total = jnp.einsum("pt,pc->tc", onehot, both, preferred_element_type=jnp.float32)
    width = values.shape[1]
    return total[:, :width] + total[:, width:]


def reduce_replicate(weight_sum, owners, factor):
    shape = weight_sum.shape
    rows = weight_sum.size // 128
    chunk = -(-rows // owners)
    flat = jnp.pad(weight_sum.reshape(rows, 128), ((0, chunk * owners - rows), (0, 0)))
    got = lax.all_to_all(flat, "vox", 0, 0, tiled=True)
    mine = (got.reshape(owners, chunk, 128).sum(axis=0) * factor).astype(jnp.bfloat16)
    spread = jnp.broadcast_to(mine[None], (owners, chunk, 128)).reshape(owners * chunk, 128)
    back = lax.all_to_all(spread, "vox", 0, 0, tiled=True)
    return back[:rows].reshape(shape)


def body(
    features,
    kernel,
    coarse_grad,
    pair_fine,
    pair_target,
    block_offset,
    target_owner,
    slot_coarse_row,
    fine_count,
):
    owners = lax.axis_size("vox")
    fine_total, width_in = features.shape
    width_out, coarse_total = coarse_grad.shape
    offsets_all = kernel.shape[0]
    targets = target_owner.shape[0]
    capacity = slot_coarse_row.shape[0] // owners
    slots = owners * capacity
    blocks = block_offset.shape[0]
    pairs = pair_fine.shape[0]
    group = pairs // blocks
    live_mask = jnp.arange(fine_total, dtype=jnp.int32) < fine_count[0]
    masked = jnp.where(live_mask[:, None], features, jnp.zeros((), features.dtype))
    fine_hot = one_hot(pair_fine, fine_total)
    target_hot = one_hot(pair_target, targets)
    gathered = jnp.dot(fine_hot, masked, preferred_element_type=jnp.float32).astype(jnp.bfloat16)
    gathered = gathered.reshape(blocks, group, width_in)
    weights = kernel[block_offset]
    partial_value = jnp.einsum(
        "bpc,boc->bpo", gathered, weights, preferred_element_type=jnp.float32
    ).reshape(pairs, width_out)
    target_part = exact_sum(target_hot, partial_value).astype(jnp.bfloat16)

    owner_of = target_owner[:, 0]
    slot_index = owner_of * capacity + owner_slots(owner_of, owners)
    slot_hot = one_hot(slot_index, slots)
    send_rows = jnp.einsum(
        "ts,to->so", slot_hot, target_part, preferred_element_type=jnp.float32
    ).astype(jnp.bfloat16)
    lane_shape = (slots * width_out // 128, 128)
    received = lax.all_to_all(
        send_rows.reshape(lane_shape), "vox", split_axis=0, concat_axis=0, tiled=True
    )
    got_rows = received.reshape(slots, width_out)
    row_hot = one_hot(slot_coarse_row, coarse_total)
    coarse = jnp.einsum("sc,so->co", row_hot, got_rows, preferred_element_type=jnp.float32)
    gate_output = jax.nn.sigmoid(coarse)
    activation = (coarse * gate_output).astype(jnp.bfloat16)
    grad_coarse = (
        coarse_grad.astype(jnp.float32).T * gate_output * (1.0 + coarse * (1.0 - gate_output))
    ).astype(jnp.bfloat16)
    back_rows = jnp.einsum(
        "sc,co->so", row_hot, grad_coarse, preferred_element_type=jnp.float32
    ).astype(jnp.bfloat16)
    returned = lax.all_to_all(
        back_rows.reshape(lane_shape), "vox", split_axis=0, concat_axis=0, tiled=True
    )
    grad_target = jnp.einsum(
        "ts,so->to", slot_hot, returned.reshape(slots, width_out), preferred_element_type=jnp.float32
    ).astype(jnp.bfloat16)
    grad_rows = jnp.einsum(
        "pt,to->po", target_hot, grad_target, preferred_element_type=jnp.float32
    ).astype(jnp.bfloat16)
    grad_rows = grad_rows.reshape(blocks, group, width_out)
    grad_in = jnp.einsum(
        "bpo,boc->bpc", grad_rows, weights, preferred_element_type=jnp.float32
    ).reshape(pairs, width_in)
    fine_sum = exact_sum(fine_hot, grad_in)
    fine_grad = lax.psum_scatter(fine_sum, "ch", scatter_dimension=1, tiled=True)
    grad_features = jnp.where(live_mask[:, None], fine_grad, jnp.zeros((), jnp.float32)).astype(
        jnp.bfloat16
    )
    grad_weight = jnp.einsum(
        "bpc,bpo->boc", gathered, grad_rows, preferred_element_type=jnp.float32
    )
    weight_sum = (
        jnp.zeros((offsets_all, width_out, width_in), jnp.float32).at[block_offset].add(grad_weight)
    )
    factor = math.sqrt(offsets_all / (blocks * group * owners))
    grad_kernel = reduce_replicate(weight_sum, owners, factor)
    return (activation.T, grad_features.T, grad_kernel)


def solution(mesh):
    in_specs = (
        P("vox", None),
        P(None, "ch", None),
        P("ch", "vox"),
        P("vox"),
        P("vox"),
        P("vox"),
        P("vox", None),
        P("vox"),
        P("vox"),
    )
    out_specs = (P("ch", "vox"), P("ch", "vox"), P(None, "ch", None))
    return jax.shard_map(body, mesh=mesh, in_specs=in_specs, out_specs=out_specs, check_vma=False)
```

```python
import math

import jax
import jax.numpy as jnp
from jax import lax
from jax.sharding import PartitionSpec as P


def owner_slots(owner_of, owners):
    labels = jnp.arange(owners, dtype=jnp.int32)
    onehot = (owner_of[:, None] == labels[None, :]).astype(jnp.int32)
    before = jnp.cumsum(onehot, axis=0) - onehot
    return jnp.sum(before * onehot, axis=1)


def one_hot(index, size):
    return (index[:, None] == jnp.arange(size, dtype=jnp.int32)[None, :]).astype(jnp.bfloat16)


def exact_sum(onehot, values):
    high = lax.reduce_precision(values, exponent_bits=8, mantissa_bits=7)
    low = values - high
    both = jnp.concatenate([high.astype(jnp.bfloat16), low.astype(jnp.bfloat16)], axis=1)
    total = jnp.einsum("pt,pc->tc", onehot, both, preferred_element_type=jnp.float32)
    width = values.shape[1]
    return total[:, :width] + total[:, width:]


VOX = ("z", "y", "core")


def staged_all_to_all(x):
    for axis, name in ((2, "core"), (1, "y"), (0, "z")):
        x = lax.all_to_all(x, name, axis, axis, tiled=True)
    return x


def reduce_replicate(weight_sum, sizes, factor):
    shape = weight_sum.shape
    owners = math.prod(sizes)
    rows = weight_sum.size // 128
    chunk = -(-rows // owners)
    flat = jnp.pad(weight_sum.reshape(rows, 128), ((0, chunk * owners - rows), (0, 0)))
    part = flat.reshape(*sizes, chunk, 128)
    for axis, name in ((2, "core"), (1, "y"), (0, "z")):
        part = lax.all_to_all(part, name, axis, axis, tiled=True).sum(axis=axis)
    mine = (part * factor).astype(jnp.bfloat16)
    for axis, name in ((0, "z"), (1, "y"), (2, "core")):
        mine = jnp.broadcast_to(mine[None], (sizes[axis],) + mine.shape)
        mine = lax.all_to_all(mine, name, 0, 0, tiled=True)
    back = jnp.transpose(mine, (2, 1, 0, 3, 4)).reshape(owners * chunk, 128)
    return back[:rows].reshape(shape)


def body(
    features,
    kernel,
    coarse_grad,
    pair_fine,
    pair_target,
    block_offset,
    target_owner,
    slot_coarse_row,
    fine_count,
):
    sizes = tuple(lax.axis_size(name) for name in VOX)
    owners = math.prod(sizes)
    fine_total, width_in = features.shape
    width_out, coarse_total = coarse_grad.shape
    offsets_all = kernel.shape[0]
    targets = target_owner.shape[0]
    capacity = slot_coarse_row.shape[0] // owners
    slots = owners * capacity
    blocks = block_offset.shape[0]
    pairs = pair_fine.shape[0]
    group = pairs // blocks
    live_mask = jnp.arange(fine_total, dtype=jnp.int32) < fine_count[0]
    masked = jnp.where(live_mask[:, None], features, jnp.zeros((), features.dtype))
    fine_hot = one_hot(pair_fine, fine_total)
    target_hot = one_hot(pair_target, targets)
    gathered = jnp.dot(fine_hot, masked, preferred_element_type=jnp.float32).astype(jnp.bfloat16)
    gathered = gathered.reshape(blocks, group, width_in)
    weights = kernel[block_offset]
    partial_value = jnp.einsum(
        "bpc,boc->bpo", gathered, weights, preferred_element_type=jnp.float32
    ).reshape(pairs, width_out)
    target_part = exact_sum(target_hot, partial_value).astype(jnp.bfloat16)

    owner_of = target_owner[:, 0]
    slot_index = owner_of * capacity + owner_slots(owner_of, owners)
    slot_hot = one_hot(slot_index, slots)
    send_rows = jnp.einsum(
        "ts,to->so", slot_hot, target_part, preferred_element_type=jnp.float32
    ).astype(jnp.bfloat16)
    lane_shape = (*sizes, capacity * width_out // 128, 128)
    received = staged_all_to_all(send_rows.reshape(lane_shape))
    got_rows = received.reshape(slots, width_out)
    row_hot = one_hot(slot_coarse_row, coarse_total)
    coarse = jnp.einsum("sc,so->co", row_hot, got_rows, preferred_element_type=jnp.float32)
    gate_output = jax.nn.sigmoid(coarse)
    activation = (coarse * gate_output).astype(jnp.bfloat16)
    grad_coarse = (
        coarse_grad.astype(jnp.float32).T * gate_output * (1.0 + coarse * (1.0 - gate_output))
    ).astype(jnp.bfloat16)
    back_rows = jnp.einsum(
        "sc,co->so", row_hot, grad_coarse, preferred_element_type=jnp.float32
    ).astype(jnp.bfloat16)
    returned = staged_all_to_all(back_rows.reshape(lane_shape))
    grad_target = jnp.einsum(
        "ts,so->to", slot_hot, returned.reshape(slots, width_out), preferred_element_type=jnp.float32
    ).astype(jnp.bfloat16)
    grad_rows = jnp.einsum(
        "pt,to->po", target_hot, grad_target, preferred_element_type=jnp.float32
    ).astype(jnp.bfloat16)
    grad_rows = grad_rows.reshape(blocks, group, width_out)
    grad_in = jnp.einsum(
        "bpo,boc->bpc", grad_rows, weights, preferred_element_type=jnp.float32
    ).reshape(pairs, width_in)
    fine_sum = exact_sum(fine_hot, grad_in)
    grad_weight = jnp.einsum(
        "bpc,bpo->boc", gathered, grad_rows, preferred_element_type=jnp.float32
    )
    weight_sum = (
        jnp.zeros((offsets_all, width_out, width_in), jnp.float32).at[block_offset].add(grad_weight)
    )
    fine_sum, weight_sum = lax.optimization_barrier((fine_sum, weight_sum))
    fine_grad = lax.psum_scatter(fine_sum, "ch", scatter_dimension=1, tiled=True)
    grad_features = jnp.where(live_mask[:, None], fine_grad, jnp.zeros((), jnp.float32)).astype(
        jnp.bfloat16
    )
    factor = math.sqrt(offsets_all / (blocks * group * owners))
    grad_kernel = reduce_replicate(weight_sum, sizes, factor)
    return (activation.T, grad_features.T, grad_kernel)


def solution(mesh):
    vox = mesh.shape["vox"]
    cores = 2
    across = 4
    split = jax.sharding.Mesh(
        mesh.devices.reshape(vox // (cores * across), across, cores, mesh.shape["ch"]),
        VOX + ("ch",),
    )
    in_specs = (
        P(VOX, None),
        P(None, "ch", None),
        P("ch", VOX),
        P(VOX),
        P(VOX),
        P(VOX),
        P(VOX, None),
        P(VOX),
        P(VOX),
    )
    out_specs = (P("ch", VOX), P("ch", VOX), P(None, "ch", None))
    return jax.shard_map(body, mesh=split, in_specs=in_specs, out_specs=out_specs, check_vma=False)
```

```python
import math

import jax
import jax.numpy as jnp
from jax import lax
from jax.sharding import PartitionSpec as P


def owner_slots(owner_of, owners):
    labels = jnp.arange(owners, dtype=jnp.int32)
    onehot = (owner_of[:, None] == labels[None, :]).astype(jnp.int32)
    before = jnp.cumsum(onehot, axis=0) - onehot
    return jnp.sum(before * onehot, axis=1)


def one_hot(index, size):
    return (index[:, None] == jnp.arange(size, dtype=jnp.int32)[None, :]).astype(jnp.bfloat16)


def exact_sum(onehot, values):
    high = lax.reduce_precision(values, exponent_bits=8, mantissa_bits=7)
    low = values - high
    both = jnp.concatenate([high.astype(jnp.bfloat16), low.astype(jnp.bfloat16)], axis=1)
    total = jnp.einsum("pt,pc->tc", onehot, both, preferred_element_type=jnp.float32)
    width = values.shape[1]
    return total[:, :width] + total[:, width:]


VOX = ("z", "y", "core")


def flat_all_to_all(x):
    return lax.all_to_all(x, VOX, 0, 0, tiled=True)


def reduce_replicate(weight_sum, sizes, factor):
    shape = weight_sum.shape
    owners = math.prod(sizes)
    rows = weight_sum.size // 128
    chunk = -(-rows // owners)
    flat = jnp.pad(weight_sum.reshape(rows, 128), ((0, chunk * owners - rows), (0, 0)))
    part = flat.reshape(*sizes, chunk, 128)
    for axis, name in ((2, "core"), (1, "y"), (0, "z")):
        part = lax.all_to_all(part, name, axis, axis, tiled=True).sum(axis=axis)
    mine = (part * factor).astype(jnp.bfloat16)
    for axis, name in ((0, "z"), (1, "y"), (2, "core")):
        mine = jnp.broadcast_to(mine[None], (sizes[axis],) + mine.shape)
        mine = lax.all_to_all(mine, name, 0, 0, tiled=True)
    back = jnp.transpose(mine, (2, 1, 0, 3, 4)).reshape(owners * chunk, 128)
    return back[:rows].reshape(shape)


def body(
    features,
    kernel,
    coarse_grad,
    pair_fine,
    pair_target,
    block_offset,
    target_owner,
    slot_coarse_row,
    fine_count,
):
    sizes = tuple(lax.axis_size(name) for name in VOX)
    owners = math.prod(sizes)
    fine_total, width_in = features.shape
    width_out, coarse_total = coarse_grad.shape
    offsets_all = kernel.shape[0]
    targets = target_owner.shape[0]
    capacity = slot_coarse_row.shape[0] // owners
    slots = owners * capacity
    blocks = block_offset.shape[0]
    pairs = pair_fine.shape[0]
    group = pairs // blocks
    live_mask = jnp.arange(fine_total, dtype=jnp.int32) < fine_count[0]
    masked = jnp.where(live_mask[:, None], features, jnp.zeros((), features.dtype))
    fine_hot = one_hot(pair_fine, fine_total)
    target_hot = one_hot(pair_target, targets)
    gathered = jnp.dot(fine_hot, masked, preferred_element_type=jnp.float32).astype(jnp.bfloat16)
    gathered = gathered.reshape(blocks, group, width_in)
    weights = kernel[block_offset]
    partial_value = jnp.einsum(
        "bpc,boc->bpo", gathered, weights, preferred_element_type=jnp.float32
    ).reshape(pairs, width_out)
    target_part = exact_sum(target_hot, partial_value).astype(jnp.bfloat16)

    owner_of = target_owner[:, 0]
    slot_index = owner_of * capacity + owner_slots(owner_of, owners)
    slot_hot = one_hot(slot_index, slots)
    send_rows = jnp.einsum(
        "ts,to->so", slot_hot, target_part, preferred_element_type=jnp.float32
    ).astype(jnp.bfloat16)
    lane_shape = (slots * width_out // 128, 128)
    received = flat_all_to_all(send_rows.reshape(lane_shape))
    got_rows = received.reshape(slots, width_out)
    row_hot = one_hot(slot_coarse_row, coarse_total)
    coarse = jnp.einsum("sc,so->co", row_hot, got_rows, preferred_element_type=jnp.float32)
    gate_output = jax.nn.sigmoid(coarse)
    activation = (coarse * gate_output).astype(jnp.bfloat16)
    grad_coarse = (
        coarse_grad.astype(jnp.float32).T * gate_output * (1.0 + coarse * (1.0 - gate_output))
    ).astype(jnp.bfloat16)
    back_rows = jnp.einsum(
        "sc,co->so", row_hot, grad_coarse, preferred_element_type=jnp.float32
    ).astype(jnp.bfloat16)
    returned = flat_all_to_all(back_rows.reshape(lane_shape))
    grad_target = jnp.einsum(
        "ts,so->to", slot_hot, returned.reshape(slots, width_out), preferred_element_type=jnp.float32
    ).astype(jnp.bfloat16)
    grad_rows = jnp.einsum(
        "pt,to->po", target_hot, grad_target, preferred_element_type=jnp.float32
    ).astype(jnp.bfloat16)
    grad_rows = grad_rows.reshape(blocks, group, width_out)
    grad_in = jnp.einsum(
        "bpo,boc->bpc", grad_rows, weights, preferred_element_type=jnp.float32
    ).reshape(pairs, width_in)
    fine_sum = exact_sum(fine_hot, grad_in)
    grad_weight = jnp.einsum(
        "bpc,bpo->boc", gathered, grad_rows, preferred_element_type=jnp.float32
    )
    weight_sum = (
        jnp.zeros((offsets_all, width_out, width_in), jnp.float32).at[block_offset].add(grad_weight)
    )
    fine_sum, weight_sum = lax.optimization_barrier((fine_sum, weight_sum))
    fine_grad = lax.psum_scatter(fine_sum, "ch", scatter_dimension=1, tiled=True)
    grad_features = jnp.where(live_mask[:, None], fine_grad, jnp.zeros((), jnp.float32)).astype(
        jnp.bfloat16
    )
    factor = math.sqrt(offsets_all / (blocks * group * owners))
    grad_kernel = reduce_replicate(weight_sum, sizes, factor)
    return (activation.T, grad_features.T, grad_kernel)


def solution(mesh):
    vox = mesh.shape["vox"]
    cores = 2
    across = 4
    split = jax.sharding.Mesh(
        mesh.devices.reshape(vox // (cores * across), across, cores, mesh.shape["ch"]),
        VOX + ("ch",),
    )
    in_specs = (
        P(VOX, None),
        P(None, "ch", None),
        P("ch", VOX),
        P(VOX),
        P(VOX),
        P(VOX),
        P(VOX, None),
        P(VOX),
        P(VOX),
    )
    out_specs = (P("ch", VOX), P("ch", VOX), P(None, "ch", None))
    return jax.shard_map(body, mesh=split, in_specs=in_specs, out_specs=out_specs, check_vma=False)
```

```python
import math

import jax
import jax.numpy as jnp
from jax import lax
from jax.sharding import PartitionSpec as P


def owner_slots(owner_of, owners):
    labels = jnp.arange(owners, dtype=jnp.int32)
    onehot = (owner_of[:, None] == labels[None, :]).astype(jnp.int32)
    before = jnp.cumsum(onehot, axis=0) - onehot
    return jnp.sum(before * onehot, axis=1)


def one_hot(index, size):
    return (index[:, None] == jnp.arange(size, dtype=jnp.int32)[None, :]).astype(jnp.bfloat16)


def exact_sum(onehot, values):
    high = lax.reduce_precision(values, exponent_bits=8, mantissa_bits=7)
    low = values - high
    both = jnp.concatenate([high.astype(jnp.bfloat16), low.astype(jnp.bfloat16)], axis=1)
    total = jnp.einsum("pt,pc->tc", onehot, both, preferred_element_type=jnp.float32)
    width = values.shape[1]
    return total[:, :width] + total[:, width:]


VOX = ("z", "y", "core")


def flat_all_to_all(x):
    return lax.all_to_all(x, VOX, 0, 0, tiled=True)


def reduce_replicate(weight_sum, sizes, factor):
    shape = weight_sum.shape
    owners = math.prod(sizes)
    near = owners // sizes[0]
    rows = weight_sum.size // 128
    chunk = -(-rows // owners)
    flat = jnp.pad(weight_sum.reshape(rows, 128), ((0, chunk * owners - rows), (0, 0)))
    part = flat.reshape(sizes[0], near, chunk, 128)
    part = lax.all_to_all(part, VOX[1:], 1, 1, tiled=True).sum(axis=1)
    part = lax.all_to_all(part, VOX[0], 0, 0, tiled=True).sum(axis=0)
    mine = (part * factor).astype(jnp.bfloat16)
    mine = jnp.broadcast_to(mine[None], (sizes[0], chunk, 128))
    mine = lax.all_to_all(mine, VOX[0], 0, 0, tiled=True)
    mine = jnp.broadcast_to(mine[None], (near, sizes[0], chunk, 128))
    mine = lax.all_to_all(mine, VOX[1:], 0, 0, tiled=True)
    back = jnp.transpose(mine, (1, 0, 2, 3)).reshape(owners * chunk, 128)
    return back[:rows].reshape(shape)


def body(
    features,
    kernel,
    coarse_grad,
    pair_fine,
    pair_target,
    block_offset,
    target_owner,
    slot_coarse_row,
    fine_count,
):
    sizes = tuple(lax.axis_size(name) for name in VOX)
    owners = math.prod(sizes)
    fine_total, width_in = features.shape
    width_out, coarse_total = coarse_grad.shape
    offsets_all = kernel.shape[0]
    targets = target_owner.shape[0]
    capacity = slot_coarse_row.shape[0] // owners
    slots = owners * capacity
    blocks = block_offset.shape[0]
    pairs = pair_fine.shape[0]
    group = pairs // blocks
    live_mask = jnp.arange(fine_total, dtype=jnp.int32) < fine_count[0]
    masked = jnp.where(live_mask[:, None], features, jnp.zeros((), features.dtype))
    fine_hot = one_hot(pair_fine, fine_total)
    target_hot = one_hot(pair_target, targets)
    gathered = jnp.dot(fine_hot, masked, preferred_element_type=jnp.float32).astype(jnp.bfloat16)
    gathered = gathered.reshape(blocks, group, width_in)
    weights = kernel[block_offset]
    partial_value = jnp.einsum(
        "bpc,boc->bpo", gathered, weights, preferred_element_type=jnp.float32
    ).reshape(pairs, width_out)
    target_part = exact_sum(target_hot, partial_value).astype(jnp.bfloat16)

    owner_of = target_owner[:, 0]
    slot_index = owner_of * capacity + owner_slots(owner_of, owners)
    slot_hot = one_hot(slot_index, slots)
    send_rows = jnp.einsum(
        "ts,to->so", slot_hot, target_part, preferred_element_type=jnp.float32
    ).astype(jnp.bfloat16)
    lane_shape = (slots * width_out // 128, 128)
    received = flat_all_to_all(send_rows.reshape(lane_shape))
    got_rows = received.reshape(slots, width_out)
    row_hot = one_hot(slot_coarse_row, coarse_total)
    coarse = jnp.einsum("sc,so->co", row_hot, got_rows, preferred_element_type=jnp.float32)
    gate_output = jax.nn.sigmoid(coarse)
    activation = (coarse * gate_output).astype(jnp.bfloat16)
    grad_coarse = (
        coarse_grad.astype(jnp.float32).T * gate_output * (1.0 + coarse * (1.0 - gate_output))
    ).astype(jnp.bfloat16)
    back_rows = jnp.einsum(
        "sc,co->so", row_hot, grad_coarse, preferred_element_type=jnp.float32
    ).astype(jnp.bfloat16)
    returned = flat_all_to_all(back_rows.reshape(lane_shape))
    grad_target = jnp.einsum(
        "ts,so->to", slot_hot, returned.reshape(slots, width_out), preferred_element_type=jnp.float32
    ).astype(jnp.bfloat16)
    grad_rows = jnp.einsum(
        "pt,to->po", target_hot, grad_target, preferred_element_type=jnp.float32
    ).astype(jnp.bfloat16)
    grad_rows = grad_rows.reshape(blocks, group, width_out)
    grad_in = jnp.einsum(
        "bpo,boc->bpc", grad_rows, weights, preferred_element_type=jnp.float32
    ).reshape(pairs, width_in)
    fine_sum = exact_sum(fine_hot, grad_in)
    grad_weight = jnp.einsum(
        "bpc,bpo->boc", gathered, grad_rows, preferred_element_type=jnp.float32
    )
    weight_sum = (
        jnp.zeros((offsets_all, width_out, width_in), jnp.float32).at[block_offset].add(grad_weight)
    )
    fine_sum, weight_sum = lax.optimization_barrier((fine_sum, weight_sum))
    fine_grad = lax.psum_scatter(fine_sum, "ch", scatter_dimension=1, tiled=True)
    grad_features = jnp.where(live_mask[:, None], fine_grad, jnp.zeros((), jnp.float32)).astype(
        jnp.bfloat16
    )
    factor = math.sqrt(offsets_all / (blocks * group * owners))
    grad_kernel = reduce_replicate(weight_sum, sizes, factor)
    return (activation.T, grad_features.T, grad_kernel)


def solution(mesh):
    vox = mesh.shape["vox"]
    cores = 2
    across = 4
    split = jax.sharding.Mesh(
        mesh.devices.reshape(vox // (cores * across), across, cores, mesh.shape["ch"]),
        VOX + ("ch",),
    )
    in_specs = (
        P(VOX, None),
        P(None, "ch", None),
        P("ch", VOX),
        P(VOX),
        P(VOX),
        P(VOX),
        P(VOX, None),
        P(VOX),
        P(VOX),
    )
    out_specs = (P("ch", VOX), P("ch", VOX), P(None, "ch", None))
    return jax.shard_map(body, mesh=split, in_specs=in_specs, out_specs=out_specs, check_vma=False)
```

```python
import math

import jax
import jax.numpy as jnp
from jax import lax
from jax.sharding import PartitionSpec as P


def owner_slots(owner_of, owners):
    labels = jnp.arange(owners, dtype=jnp.int32)
    onehot = (owner_of[:, None] == labels[None, :]).astype(jnp.int32)
    before = jnp.cumsum(onehot, axis=0) - onehot
    return jnp.sum(before * onehot, axis=1)


def one_hot(index, size):
    return (index[:, None] == jnp.arange(size, dtype=jnp.int32)[None, :]).astype(jnp.bfloat16)


def exact_sum(onehot, values):
    high = lax.reduce_precision(values, exponent_bits=8, mantissa_bits=7)
    low = values - high
    both = jnp.concatenate([high.astype(jnp.bfloat16), low.astype(jnp.bfloat16)], axis=1)
    total = jnp.einsum("pt,pc->tc", onehot, both, preferred_element_type=jnp.float32)
    width = values.shape[1]
    return total[:, :width] + total[:, width:]


VOX = ("z", "y", "core")


def flat_all_to_all(x):
    return lax.all_to_all(x, VOX, 0, 0, tiled=True)


def reduce_replicate(weight_sum, sizes, factor):
    shape = weight_sum.shape
    owners = math.prod(sizes)
    near = owners // sizes[0]
    rows = weight_sum.size // 128
    chunk = -(-rows // owners)
    flat = jnp.pad(weight_sum.reshape(rows, 128), ((0, chunk * owners - rows), (0, 0)))
    part = flat.reshape(sizes[0], near, chunk, 128)
    part = lax.all_to_all(part, VOX[1:], 1, 1, tiled=True).sum(axis=1)
    part = lax.all_to_all(part, VOX[0], 0, 0, tiled=True).sum(axis=0)
    mine = (part * factor).astype(jnp.bfloat16)
    mine = jnp.broadcast_to(mine[None], (sizes[0], chunk, 128))
    mine = lax.all_to_all(mine, VOX[0], 0, 0, tiled=True)
    mine = jnp.broadcast_to(mine[None], (near, sizes[0], chunk, 128))
    mine = lax.all_to_all(mine, VOX[1:], 0, 0, tiled=True)
    back = jnp.transpose(mine, (1, 0, 2, 3)).reshape(owners * chunk, 128)
    return back[:rows].reshape(shape)


def body(
    features,
    kernel,
    coarse_grad,
    pair_fine,
    pair_target,
    block_offset,
    target_owner,
    slot_coarse_row,
    fine_count,
):
    sizes = tuple(lax.axis_size(name) for name in VOX)
    owners = math.prod(sizes)
    fine_total, width_in = features.shape
    width_out, coarse_total = coarse_grad.shape
    offsets_all = kernel.shape[0]
    targets = target_owner.shape[0]
    capacity = slot_coarse_row.shape[0] // owners
    slots = owners * capacity
    blocks = block_offset.shape[0]
    pairs = pair_fine.shape[0]
    group = pairs // blocks
    live_mask = jnp.arange(fine_total, dtype=jnp.int32) < fine_count[0]
    masked = jnp.where(live_mask[:, None], features, jnp.zeros((), features.dtype))
    fine_hot = one_hot(pair_fine, fine_total)
    target_hot = one_hot(pair_target, targets)
    gathered = jnp.dot(fine_hot, masked, preferred_element_type=jnp.float32).astype(jnp.bfloat16)
    gathered = gathered.reshape(blocks, group, width_in)
    weights = kernel[block_offset]
    partial_value = jnp.einsum(
        "bpc,boc->bpo", gathered, weights, preferred_element_type=jnp.float32
    ).reshape(pairs, width_out)
    target_part = exact_sum(target_hot, partial_value).astype(jnp.bfloat16)

    owner_of = target_owner[:, 0]
    slot_index = owner_of * capacity + owner_slots(owner_of, owners)
    slot_hot = one_hot(slot_index, slots)
    send_rows = jnp.einsum(
        "ts,to->so", slot_hot, target_part, preferred_element_type=jnp.float32
    ).astype(jnp.bfloat16)
    lane_shape = (slots * width_out // 128, 128)
    received = flat_all_to_all(send_rows.reshape(lane_shape))
    got_rows = received.reshape(slots, width_out)
    row_hot = one_hot(slot_coarse_row, coarse_total)
    coarse = jnp.einsum("sc,so->co", row_hot, got_rows, preferred_element_type=jnp.float32)
    gate_output = jax.nn.sigmoid(coarse)
    activation = (coarse * gate_output).astype(jnp.bfloat16)
    grad_coarse = (
        coarse_grad.astype(jnp.float32).T * gate_output * (1.0 + coarse * (1.0 - gate_output))
    ).astype(jnp.bfloat16)
    back_rows = jnp.einsum(
        "sc,co->so", row_hot, grad_coarse, preferred_element_type=jnp.float32
    ).astype(jnp.bfloat16)
    returned = flat_all_to_all(back_rows.reshape(lane_shape))
    grad_target = jnp.einsum(
        "ts,so->to", slot_hot, returned.reshape(slots, width_out), preferred_element_type=jnp.float32
    ).astype(jnp.bfloat16)
    grad_rows = jnp.einsum(
        "pt,to->po", target_hot, grad_target, preferred_element_type=jnp.float32
    ).astype(jnp.bfloat16)
    grad_rows = grad_rows.reshape(blocks, group, width_out)
    grad_in = jnp.einsum(
        "bpo,boc->bpc", grad_rows, weights, preferred_element_type=jnp.float32
    ).reshape(pairs, width_in)
    fine_sum = exact_sum(fine_hot, grad_in)
    grad_weight = jnp.einsum(
        "bpc,bpo->boc", gathered, grad_rows, preferred_element_type=jnp.float32
    )
    offset_hot = one_hot(block_offset, offsets_all).astype(jnp.float32)
    weight_sum = jnp.einsum(
        "bk,boc->koc", offset_hot, grad_weight, precision=lax.Precision.HIGHEST
    )
    fine_grad = lax.psum_scatter(fine_sum, "ch", scatter_dimension=1, tiled=True)
    grad_features = jnp.where(live_mask[:, None], fine_grad, jnp.zeros((), jnp.float32)).astype(
        jnp.bfloat16
    )
    factor = math.sqrt(offsets_all / (blocks * group * owners))
    grad_kernel = reduce_replicate(weight_sum, sizes, factor)
    return (activation.T, grad_features.T, grad_kernel)


def solution(mesh):
    vox = mesh.shape["vox"]
    cores = 2
    across = 4
    split = jax.sharding.Mesh(
        mesh.devices.reshape(vox // (cores * across), across, cores, mesh.shape["ch"]),
        VOX + ("ch",),
    )
    in_specs = (
        P(VOX, None),
        P(None, "ch", None),
        P("ch", VOX),
        P(VOX),
        P(VOX),
        P(VOX),
        P(VOX, None),
        P(VOX),
        P(VOX),
    )
    out_specs = (P("ch", VOX), P("ch", VOX), P(None, "ch", None))
    return jax.shard_map(body, mesh=split, in_specs=in_specs, out_specs=out_specs, check_vma=False)
```

```python
import math

import jax
import jax.numpy as jnp
from jax import lax
from jax.sharding import PartitionSpec as P


def owner_slots(owner_of, owners):
    labels = jnp.arange(owners, dtype=jnp.int32)
    onehot = (owner_of[:, None] == labels[None, :]).astype(jnp.int32)
    before = jnp.cumsum(onehot, axis=0) - onehot
    return jnp.sum(before * onehot, axis=1)


def one_hot(index, size):
    return (index[:, None] == jnp.arange(size, dtype=jnp.int32)[None, :]).astype(jnp.bfloat16)


def exact_sum(onehot, values):
    high = lax.reduce_precision(values, exponent_bits=8, mantissa_bits=7)
    low = values - high
    both = jnp.concatenate([high.astype(jnp.bfloat16), low.astype(jnp.bfloat16)], axis=1)
    total = jnp.einsum("pt,pc->tc", onehot, both, preferred_element_type=jnp.float32)
    width = values.shape[1]
    return total[:, :width] + total[:, width:]


VOX = ("z", "y", "core")


def flat_all_to_all(x):
    return lax.all_to_all(x, VOX, 0, 0, tiled=True)


def reduce_replicate(weight_sum, sizes, factor, rows):
    owners = math.prod(sizes)
    near = owners // sizes[0]
    width = weight_sum.shape[-1]
    chunk = weight_sum.size // (width * owners)
    part = weight_sum.reshape(near, sizes[0], chunk, width)
    part = lax.all_to_all(part, VOX[1:], 0, 0, tiled=True).sum(axis=0)
    part = lax.all_to_all(part, VOX[0], 0, 0, tiled=True).sum(axis=0)
    mine = (part * factor).astype(jnp.bfloat16)
    mine = jnp.broadcast_to(mine[None], (sizes[0], chunk, width))
    mine = lax.all_to_all(mine, VOX[0], 0, 0, tiled=True)
    mine = jnp.broadcast_to(mine[None], (near, sizes[0], chunk, width))
    mine = lax.all_to_all(mine, VOX[1:], 0, 0, tiled=True)
    back = mine.reshape(owners * chunk, width)
    return back[:rows].reshape((-1,) + weight_sum.shape[1:])


def body(
    features,
    kernel,
    coarse_grad,
    pair_fine,
    pair_target,
    block_offset,
    target_owner,
    slot_coarse_row,
    fine_count,
):
    sizes = tuple(lax.axis_size(name) for name in VOX)
    owners = math.prod(sizes)
    fine_total, width_in = features.shape
    width_out, coarse_total = coarse_grad.shape
    offsets_all = kernel.shape[0]
    targets = target_owner.shape[0]
    capacity = slot_coarse_row.shape[0] // owners
    slots = owners * capacity
    blocks = block_offset.shape[0]
    pairs = pair_fine.shape[0]
    group = pairs // blocks
    live_mask = jnp.arange(fine_total, dtype=jnp.int32) < fine_count[0]
    masked = jnp.where(live_mask[:, None], features, jnp.zeros((), features.dtype))
    fine_hot = one_hot(pair_fine, fine_total)
    target_hot = one_hot(pair_target, targets)
    gathered = jnp.dot(fine_hot, masked, preferred_element_type=jnp.float32).astype(jnp.bfloat16)
    gathered = gathered.reshape(blocks, group, width_in)
    weights = kernel[block_offset]
    partial_value = jnp.einsum(
        "bpc,boc->bpo", gathered, weights, preferred_element_type=jnp.float32
    ).reshape(pairs, width_out)
    target_part = exact_sum(target_hot, partial_value).astype(jnp.bfloat16)

    owner_of = target_owner[:, 0]
    slot_index = owner_of * capacity + owner_slots(owner_of, owners)
    slot_hot = one_hot(slot_index, slots)
    send_rows = jnp.einsum(
        "ts,to->so", slot_hot, target_part, preferred_element_type=jnp.float32
    ).astype(jnp.bfloat16)
    lane_shape = (slots * width_out // 128, 128)
    received = flat_all_to_all(send_rows.reshape(lane_shape))
    got_rows = received.reshape(slots, width_out)
    row_hot = one_hot(slot_coarse_row, coarse_total)
    coarse = jnp.einsum("sc,so->co", row_hot, got_rows, preferred_element_type=jnp.float32)
    gate_output = jax.nn.sigmoid(coarse)
    activation = (coarse * gate_output).astype(jnp.bfloat16)
    grad_coarse = (
        coarse_grad.astype(jnp.float32).T * gate_output * (1.0 + coarse * (1.0 - gate_output))
    ).astype(jnp.bfloat16)
    back_rows = jnp.einsum(
        "sc,co->so", row_hot, grad_coarse, preferred_element_type=jnp.float32
    ).astype(jnp.bfloat16)
    returned = flat_all_to_all(back_rows.reshape(lane_shape))
    grad_target = jnp.einsum(
        "ts,so->to", slot_hot, returned.reshape(slots, width_out), preferred_element_type=jnp.float32
    ).astype(jnp.bfloat16)
    grad_rows = jnp.einsum(
        "pt,to->po", target_hot, grad_target, preferred_element_type=jnp.float32
    ).astype(jnp.bfloat16)
    grad_rows = grad_rows.reshape(blocks, group, width_out)
    grad_in = jnp.einsum(
        "bpo,boc->bpc", grad_rows, weights, preferred_element_type=jnp.float32
    ).reshape(pairs, width_in)
    fine_sum = exact_sum(fine_hot, grad_in)
    grad_weight = jnp.einsum(
        "bpc,bpo->boc", gathered, grad_rows, preferred_element_type=jnp.float32
    )
    rows_all = offsets_all * width_out
    step = owners * 8
    padded = -(-rows_all // step) * step // width_out
    offset_hot = one_hot(block_offset, padded).astype(jnp.float32)
    weight_sum = jnp.einsum(
        "bk,boc->koc", offset_hot, grad_weight, precision=lax.Precision.HIGHEST
    )
    fine_grad = lax.psum_scatter(fine_sum, "ch", scatter_dimension=1, tiled=True)
    grad_features = jnp.where(live_mask[:, None], fine_grad, jnp.zeros((), jnp.float32)).astype(
        jnp.bfloat16
    )
    factor = math.sqrt(offsets_all / (blocks * group * owners))
    grad_kernel = reduce_replicate(weight_sum, sizes, factor, rows_all)
    return (activation.T, grad_features.T, grad_kernel)


def solution(mesh):
    vox = mesh.shape["vox"]
    cores = 2
    across = 4
    split = jax.sharding.Mesh(
        mesh.devices.reshape(vox // (cores * across), across, cores, mesh.shape["ch"]),
        VOX + ("ch",),
    )
    in_specs = (
        P(VOX, None),
        P(None, "ch", None),
        P("ch", VOX),
        P(VOX),
        P(VOX),
        P(VOX),
        P(VOX, None),
        P(VOX),
        P(VOX),
    )
    out_specs = (P("ch", VOX), P("ch", VOX), P(None, "ch", None))
    return jax.shard_map(body, mesh=split, in_specs=in_specs, out_specs=out_specs, check_vma=False)
```

```python
import math

import jax
import jax.numpy as jnp
from jax import lax
from jax.sharding import PartitionSpec as P


def owner_slots(owner_of, owners):
    labels = jnp.arange(owners, dtype=jnp.int32)
    onehot = (owner_of[:, None] == labels[None, :]).astype(jnp.int32)
    before = jnp.cumsum(onehot, axis=0) - onehot
    return jnp.sum(before * onehot, axis=1)


def one_hot(index, size):
    return (index[:, None] == jnp.arange(size, dtype=jnp.int32)[None, :]).astype(jnp.bfloat16)


def exact_sum(onehot, values):
    high = lax.reduce_precision(values, exponent_bits=8, mantissa_bits=7)
    low = values - high
    both = jnp.concatenate([high.astype(jnp.bfloat16), low.astype(jnp.bfloat16)], axis=1)
    total = jnp.einsum("pt,pc->tc", onehot, both, preferred_element_type=jnp.float32)
    width = values.shape[1]
    return total[:, :width] + total[:, width:]


VOX = ("z", "y", "core")


def flat_all_to_all(x):
    return lax.all_to_all(x, VOX, 0, 0, tiled=True)


def exact_sum_t(onehot, values):
    high = lax.reduce_precision(values, exponent_bits=8, mantissa_bits=7)
    low = values - high
    both = jnp.concatenate([high.astype(jnp.bfloat16), low.astype(jnp.bfloat16)], axis=1)
    total = jnp.einsum("pc,pt->ct", both, onehot, preferred_element_type=jnp.float32)
    width = values.shape[1]
    return total[:width] + total[width:]


def reduce_replicate(weight_sum, sizes, factor, rows):
    owners = math.prod(sizes)
    near = owners // sizes[0]
    width = weight_sum.shape[-1]
    chunk = weight_sum.size // (width * owners)
    part = weight_sum.reshape(near, sizes[0], chunk, width)
    part = lax.all_to_all(part, VOX[1:], 0, 0, tiled=True).sum(axis=0)
    part = lax.all_to_all(part, VOX[0], 0, 0, tiled=True).sum(axis=0)
    mine = (part * factor).astype(jnp.bfloat16)
    mine = jnp.broadcast_to(mine[None], (sizes[0], chunk, width))
    mine = lax.all_to_all(mine, VOX[0], 0, 0, tiled=True)
    mine = jnp.broadcast_to(mine[None], (near, sizes[0], chunk, width))
    mine = lax.all_to_all(mine, VOX[1:], 0, 0, tiled=True)
    back = mine.reshape(owners * chunk, width)
    return back[:rows].reshape((-1,) + weight_sum.shape[1:])


def body(
    features,
    kernel,
    coarse_grad,
    pair_fine,
    pair_target,
    block_offset,
    target_owner,
    slot_coarse_row,
    fine_count,
):
    sizes = tuple(lax.axis_size(name) for name in VOX)
    owners = math.prod(sizes)
    fine_total, width_in = features.shape
    width_out, coarse_total = coarse_grad.shape
    offsets_all = kernel.shape[0]
    targets = target_owner.shape[0]
    capacity = slot_coarse_row.shape[0] // owners
    slots = owners * capacity
    blocks = block_offset.shape[0]
    pairs = pair_fine.shape[0]
    group = pairs // blocks
    live_mask = jnp.arange(fine_total, dtype=jnp.int32) < fine_count[0]
    masked = jnp.where(live_mask[:, None], features, jnp.zeros((), features.dtype))
    fine_hot = one_hot(pair_fine, fine_total)
    target_hot = one_hot(pair_target, targets)
    gathered = jnp.dot(fine_hot, masked, preferred_element_type=jnp.float32).astype(jnp.bfloat16)
    gathered = gathered.reshape(blocks, group, width_in)
    weights = kernel[block_offset]
    partial_value = jnp.einsum(
        "bpc,boc->bpo", gathered, weights, preferred_element_type=jnp.float32
    ).reshape(pairs, width_out)
    target_part = exact_sum(target_hot, partial_value).astype(jnp.bfloat16)

    owner_of = target_owner[:, 0]
    slot_index = owner_of * capacity + owner_slots(owner_of, owners)
    slot_hot = one_hot(slot_index, slots)
    send_rows = jnp.einsum(
        "ts,to->so", slot_hot, target_part, preferred_element_type=jnp.float32
    ).astype(jnp.bfloat16)
    lane_shape = (slots * width_out // 128, 128)
    received = flat_all_to_all(send_rows.reshape(lane_shape))
    got_rows = received.reshape(slots, width_out)
    row_hot = one_hot(slot_coarse_row, coarse_total)
    coarse = jnp.einsum("sc,so->co", row_hot, got_rows, preferred_element_type=jnp.float32)
    gate_output = jax.nn.sigmoid(coarse)
    activation = (coarse * gate_output).astype(jnp.bfloat16)
    grad_coarse = (
        coarse_grad.astype(jnp.float32).T * gate_output * (1.0 + coarse * (1.0 - gate_output))
    ).astype(jnp.bfloat16)
    back_rows = jnp.einsum(
        "sc,co->so", row_hot, grad_coarse, preferred_element_type=jnp.float32
    ).astype(jnp.bfloat16)
    returned = flat_all_to_all(back_rows.reshape(lane_shape))
    grad_target = jnp.einsum(
        "ts,so->to", slot_hot, returned.reshape(slots, width_out), preferred_element_type=jnp.float32
    ).astype(jnp.bfloat16)
    grad_rows = jnp.einsum(
        "pt,to->po", target_hot, grad_target, preferred_element_type=jnp.float32
    ).astype(jnp.bfloat16)
    grad_rows = grad_rows.reshape(blocks, group, width_out)
    grad_in = jnp.einsum(
        "bpo,boc->bpc", grad_rows, weights, preferred_element_type=jnp.float32
    ).reshape(pairs, width_in)
    fine_sum = exact_sum_t(fine_hot, grad_in)
    grad_weight = jnp.einsum(
        "bpc,bpo->boc", gathered, grad_rows, preferred_element_type=jnp.float32
    )
    rows_all = offsets_all * width_out
    step = owners * 8
    padded = -(-rows_all // step) * step // width_out
    offset_hot = one_hot(block_offset, padded).astype(jnp.float32)
    weight_sum = jnp.einsum(
        "bk,boc->koc", offset_hot, grad_weight, precision=lax.Precision.HIGHEST
    )
    groups = lax.axis_size("ch")
    fine_parts = fine_sum.reshape(groups, width_in // groups, fine_total)
    fine_grad = lax.all_to_all(fine_parts, "ch", 0, 0, tiled=True).sum(axis=0)
    grad_features = jnp.where(live_mask[None, :], fine_grad, jnp.zeros((), jnp.float32)).astype(
        jnp.bfloat16
    )
    factor = math.sqrt(offsets_all / (blocks * group * owners))
    grad_kernel = reduce_replicate(weight_sum, sizes, factor, rows_all)
    return (activation.T, grad_features, grad_kernel)


def solution(mesh):
    vox = mesh.shape["vox"]
    cores = 2
    across = 4
    split = jax.sharding.Mesh(
        mesh.devices.reshape(vox // (cores * across), across, cores, mesh.shape["ch"]),
        VOX + ("ch",),
    )
    in_specs = (
        P(VOX, None),
        P(None, "ch", None),
        P("ch", VOX),
        P(VOX),
        P(VOX),
        P(VOX),
        P(VOX, None),
        P(VOX),
        P(VOX),
    )
    out_specs = (P("ch", VOX), P("ch", VOX), P(None, "ch", None))
    return jax.shard_map(body, mesh=split, in_specs=in_specs, out_specs=out_specs, check_vma=False)
```

```python
import math

import jax
import jax.numpy as jnp
from jax import lax
from jax.sharding import PartitionSpec as P


def owner_slots(owner_of, owners):
    labels = jnp.arange(owners, dtype=jnp.int32)
    onehot = (owner_of[:, None] == labels[None, :]).astype(jnp.int32)
    before = jnp.cumsum(onehot, axis=0) - onehot
    return jnp.sum(before * onehot, axis=1)


def one_hot(index, size):
    return (index[:, None] == jnp.arange(size, dtype=jnp.int32)[None, :]).astype(jnp.bfloat16)


def exact_sum(onehot, values):
    high = lax.reduce_precision(values, exponent_bits=8, mantissa_bits=7)
    low = values - high
    both = jnp.concatenate([high.astype(jnp.bfloat16), low.astype(jnp.bfloat16)], axis=1)
    total = jnp.einsum("pt,pc->tc", onehot, both, preferred_element_type=jnp.float32)
    width = values.shape[1]
    return total[:, :width] + total[:, width:]


VOX = ("z", "y", "core")


def flat_all_to_all(x):
    return lax.all_to_all(x, VOX, 0, 0, tiled=True)


def exact_sum_t(onehot, values):
    high = lax.reduce_precision(values, exponent_bits=8, mantissa_bits=7)
    low = values - high
    both = jnp.concatenate([high.astype(jnp.bfloat16), low.astype(jnp.bfloat16)], axis=1)
    total = jnp.einsum("pc,pt->ct", both, onehot, preferred_element_type=jnp.float32)
    width = values.shape[1]
    return total[:width] + total[width:]


def reduce_replicate(weight_sum, sizes, factor, rows):
    owners = math.prod(sizes)
    near = owners // sizes[0]
    width = weight_sum.shape[-1]
    chunk = weight_sum.size // (width * owners)
    part = weight_sum.reshape(near, sizes[0], chunk, width)
    part = lax.all_to_all(part.astype(jnp.bfloat16), VOX[1:], 0, 0, tiled=True)
    part = part.astype(jnp.float32).sum(axis=0)
    part = lax.all_to_all(part, VOX[0], 0, 0, tiled=True).sum(axis=0)
    mine = (part * factor).astype(jnp.bfloat16)
    mine = jnp.broadcast_to(mine[None], (sizes[0], chunk, width))
    mine = lax.all_to_all(mine, VOX[0], 0, 0, tiled=True)
    mine = jnp.broadcast_to(mine[None], (near, sizes[0], chunk, width))
    mine = lax.all_to_all(mine, VOX[1:], 0, 0, tiled=True)
    back = mine.reshape(owners * chunk, width)
    return back[:rows].reshape((-1,) + weight_sum.shape[1:])


def body(
    features,
    kernel,
    coarse_grad,
    pair_fine,
    pair_target,
    block_offset,
    target_owner,
    slot_coarse_row,
    fine_count,
):
    sizes = tuple(lax.axis_size(name) for name in VOX)
    owners = math.prod(sizes)
    fine_total, width_in = features.shape
    width_out, coarse_total = coarse_grad.shape
    offsets_all = kernel.shape[0]
    targets = target_owner.shape[0]
    capacity = slot_coarse_row.shape[0] // owners
    slots = owners * capacity
    blocks = block_offset.shape[0]
    pairs = pair_fine.shape[0]
    group = pairs // blocks
    live_mask = jnp.arange(fine_total, dtype=jnp.int32) < fine_count[0]
    masked = jnp.where(live_mask[:, None], features, jnp.zeros((), features.dtype))
    fine_hot = one_hot(pair_fine, fine_total)
    target_hot = one_hot(pair_target, targets)
    gathered = jnp.dot(fine_hot, masked, preferred_element_type=jnp.float32).astype(jnp.bfloat16)
    gathered = gathered.reshape(blocks, group, width_in)
    weights = kernel[block_offset]
    partial_value = jnp.einsum(
        "bpc,boc->bpo", gathered, weights, preferred_element_type=jnp.float32
    ).reshape(pairs, width_out)
    target_part = exact_sum(target_hot, partial_value).astype(jnp.bfloat16)

    owner_of = target_owner[:, 0]
    slot_index = owner_of * capacity + owner_slots(owner_of, owners)
    slot_hot = one_hot(slot_index, slots)
    send_rows = jnp.einsum(
        "ts,to->so", slot_hot, target_part, preferred_element_type=jnp.float32
    ).astype(jnp.bfloat16)
    lane_shape = (slots * width_out // 128, 128)
    received = flat_all_to_all(send_rows.reshape(lane_shape))
    got_rows = received.reshape(slots, width_out)
    row_hot = one_hot(slot_coarse_row, coarse_total)
    coarse = jnp.einsum("sc,so->co", row_hot, got_rows, preferred_element_type=jnp.float32)
    gate_output = jax.nn.sigmoid(coarse)
    activation = (coarse * gate_output).astype(jnp.bfloat16)
    grad_coarse = (
        coarse_grad.astype(jnp.float32).T * gate_output * (1.0 + coarse * (1.0 - gate_output))
    ).astype(jnp.bfloat16)
    back_rows = jnp.einsum(
        "sc,co->so", row_hot, grad_coarse, preferred_element_type=jnp.float32
    ).astype(jnp.bfloat16)
    returned = flat_all_to_all(back_rows.reshape(lane_shape))
    grad_target = jnp.einsum(
        "ts,so->to", slot_hot, returned.reshape(slots, width_out), preferred_element_type=jnp.float32
    ).astype(jnp.bfloat16)
    grad_rows = jnp.einsum(
        "pt,to->po", target_hot, grad_target, preferred_element_type=jnp.float32
    ).astype(jnp.bfloat16)
    grad_rows = grad_rows.reshape(blocks, group, width_out)
    grad_in = jnp.einsum(
        "bpo,boc->bpc", grad_rows, weights, preferred_element_type=jnp.float32
    ).reshape(pairs, width_in)
    fine_sum = exact_sum_t(fine_hot, grad_in)
    grad_weight = jnp.einsum(
        "bpc,bpo->boc", gathered, grad_rows, preferred_element_type=jnp.float32
    )
    rows_all = offsets_all * width_out
    step = owners * 8
    padded = -(-rows_all // step) * step // width_out
    offset_hot = one_hot(block_offset, padded).astype(jnp.float32)
    weight_sum = jnp.einsum(
        "bk,boc->koc", offset_hot, grad_weight, precision=lax.Precision.HIGHEST
    )
    groups = lax.axis_size("ch")
    fine_parts = fine_sum.reshape(groups, width_in // groups, fine_total)
    fine_grad = lax.all_to_all(fine_parts, "ch", 0, 0, tiled=True).sum(axis=0)
    grad_features = jnp.where(live_mask[None, :], fine_grad, jnp.zeros((), jnp.float32)).astype(
        jnp.bfloat16
    )
    factor = math.sqrt(offsets_all / (blocks * group * owners))
    grad_kernel = reduce_replicate(weight_sum, sizes, factor, rows_all)
    return (activation.T, grad_features, grad_kernel)


def solution(mesh):
    vox = mesh.shape["vox"]
    cores = 2
    across = 4
    split = jax.sharding.Mesh(
        mesh.devices.reshape(vox // (cores * across), across, cores, mesh.shape["ch"]),
        VOX + ("ch",),
    )
    in_specs = (
        P(VOX, None),
        P(None, "ch", None),
        P("ch", VOX),
        P(VOX),
        P(VOX),
        P(VOX),
        P(VOX, None),
        P(VOX),
        P(VOX),
    )
    out_specs = (P("ch", VOX), P("ch", VOX), P(None, "ch", None))
    return jax.shard_map(body, mesh=split, in_specs=in_specs, out_specs=out_specs, check_vma=False)
```

```python
import math

import jax
import jax.numpy as jnp
from jax import lax
from jax.sharding import PartitionSpec as P


def owner_slots(owner_of, owners):
    labels = jnp.arange(owners, dtype=jnp.int32)
    onehot = (owner_of[:, None] == labels[None, :]).astype(jnp.int32)
    before = jnp.cumsum(onehot, axis=0) - onehot
    return jnp.sum(before * onehot, axis=1)


def one_hot(index, size):
    return (index[:, None] == jnp.arange(size, dtype=jnp.int32)[None, :]).astype(jnp.bfloat16)


def exact_sum(onehot, values):
    high = lax.reduce_precision(values, exponent_bits=8, mantissa_bits=7)
    low = values - high
    both = jnp.concatenate([high.astype(jnp.bfloat16), low.astype(jnp.bfloat16)], axis=1)
    total = jnp.einsum("pt,pc->tc", onehot, both, preferred_element_type=jnp.float32)
    width = values.shape[1]
    return total[:, :width] + total[:, width:]


VOX = ("z", "y", "core")


def flat_all_to_all(x):
    return lax.all_to_all(x, VOX, 0, 0, tiled=True)


def exact_sum_t(onehot, values):
    high = lax.reduce_precision(values, exponent_bits=8, mantissa_bits=7)
    low = values - high
    both = jnp.concatenate([high.astype(jnp.bfloat16), low.astype(jnp.bfloat16)], axis=1)
    total = jnp.einsum("pc,pt->ct", both, onehot, preferred_element_type=jnp.float32)
    width = values.shape[1]
    return total[:width] + total[width:]


def reduce_replicate(weight_sum, sizes, factor, rows):
    owners = math.prod(sizes)
    near = owners // sizes[0]
    width = weight_sum.shape[-1]
    chunk = weight_sum.size // (width * owners)
    part = weight_sum.reshape(near, sizes[0], chunk, width)
    part = lax.all_to_all(part.astype(jnp.bfloat16), VOX[1:], 0, 0, tiled=True)
    part = part.astype(jnp.float32).sum(axis=0)
    part = lax.all_to_all(part, VOX[0], 0, 0, tiled=True).sum(axis=0)
    mine = (part * factor).astype(jnp.bfloat16)
    mine = jnp.broadcast_to(mine[None], (sizes[0], chunk, width))
    mine = lax.all_to_all(mine, VOX[0], 0, 0, tiled=True)
    mine = jnp.broadcast_to(mine[None], (near, sizes[0], chunk, width))
    mine = lax.all_to_all(mine, VOX[1:], 0, 0, tiled=True)
    back = mine.reshape(owners * chunk, width)
    return back[:rows].reshape((-1,) + weight_sum.shape[1:])


def body(
    features,
    kernel,
    coarse_grad,
    pair_fine,
    pair_target,
    block_offset,
    target_owner,
    slot_coarse_row,
    fine_count,
):
    sizes = tuple(lax.axis_size(name) for name in VOX)
    owners = math.prod(sizes)
    fine_total, width_in = features.shape
    width_out, coarse_total = coarse_grad.shape
    offsets_all = kernel.shape[0]
    targets = target_owner.shape[0]
    capacity = slot_coarse_row.shape[0] // owners
    slots = owners * capacity
    blocks = block_offset.shape[0]
    pairs = pair_fine.shape[0]
    group = pairs // blocks
    live_mask = jnp.arange(fine_total, dtype=jnp.int32) < fine_count[0]
    masked = jnp.where(live_mask[:, None], features, jnp.zeros((), features.dtype))
    fine_hot = one_hot(pair_fine, fine_total)
    target_hot = one_hot(pair_target, targets)
    gathered = jnp.dot(fine_hot, masked, preferred_element_type=jnp.float32).astype(jnp.bfloat16)
    gathered = gathered.reshape(blocks, group, width_in)
    weights = kernel[block_offset]
    partial_value = jnp.einsum(
        "bpc,boc->bpo", gathered, weights, preferred_element_type=jnp.float32
    ).reshape(pairs, width_out)
    target_part = exact_sum(target_hot, partial_value).astype(jnp.bfloat16)

    owner_of = target_owner[:, 0]
    slot_index = owner_of * capacity + owner_slots(owner_of, owners)
    slot_hot = one_hot(slot_index, slots)
    send_rows = jnp.einsum(
        "ts,to->so", slot_hot, target_part, preferred_element_type=jnp.float32
    ).astype(jnp.bfloat16)
    lane_shape = (slots * width_out // 128, 128)
    received = flat_all_to_all(send_rows.reshape(lane_shape))
    got_rows = received.reshape(slots, width_out)
    row_hot = one_hot(slot_coarse_row, coarse_total)
    coarse = jnp.einsum("sc,so->co", row_hot, got_rows, preferred_element_type=jnp.float32)
    gate_output = jax.nn.sigmoid(coarse)
    activation = (coarse * gate_output).astype(jnp.bfloat16)
    grad_coarse = (
        coarse_grad.astype(jnp.float32).T * gate_output * (1.0 + coarse * (1.0 - gate_output))
    ).astype(jnp.bfloat16)
    back_rows = jnp.einsum(
        "sc,co->so", row_hot, grad_coarse, preferred_element_type=jnp.float32
    ).astype(jnp.bfloat16)
    returned = flat_all_to_all(back_rows.reshape(lane_shape))
    grad_target = jnp.einsum(
        "ts,so->to", slot_hot, returned.reshape(slots, width_out), preferred_element_type=jnp.float32
    ).astype(jnp.bfloat16)
    grad_rows = jnp.einsum(
        "pt,to->po", target_hot, grad_target, preferred_element_type=jnp.float32
    ).astype(jnp.bfloat16)
    grad_rows = grad_rows.reshape(blocks, group, width_out)
    grad_in = jnp.einsum(
        "bpo,boc->bpc", grad_rows, weights, preferred_element_type=jnp.float32
    ).reshape(pairs, width_in)
    fine_sum = exact_sum_t(fine_hot, grad_in)
    grad_weight = jnp.einsum(
        "bpc,bpo->boc", gathered, grad_rows, preferred_element_type=jnp.float32
    )
    rows_all = offsets_all * width_out
    step = owners * 8
    padded = -(-rows_all // step) * step // width_out
    offset_hot = one_hot(block_offset, padded).astype(jnp.float32)
    weight_sum = jnp.einsum(
        "bk,boc->koc", offset_hot, grad_weight, precision=lax.Precision.HIGHEST
    )
    groups = lax.axis_size("ch")
    fine_parts = fine_sum.reshape(groups, width_in // groups, fine_total)
    fine_parts = lax.all_to_all(fine_parts.astype(jnp.bfloat16), "ch", 0, 0, tiled=True)
    fine_grad = fine_parts.astype(jnp.float32).sum(axis=0)
    grad_features = jnp.where(live_mask[None, :], fine_grad, jnp.zeros((), jnp.float32)).astype(
        jnp.bfloat16
    )
    factor = math.sqrt(offsets_all / (blocks * group * owners))
    grad_kernel = reduce_replicate(weight_sum, sizes, factor, rows_all)
    return (activation.T, grad_features, grad_kernel)


def solution(mesh):
    vox = mesh.shape["vox"]
    cores = 2
    across = 4
    split = jax.sharding.Mesh(
        mesh.devices.reshape(vox // (cores * across), across, cores, mesh.shape["ch"]),
        VOX + ("ch",),
    )
    in_specs = (
        P(VOX, None),
        P(None, "ch", None),
        P("ch", VOX),
        P(VOX),
        P(VOX),
        P(VOX),
        P(VOX, None),
        P(VOX),
        P(VOX),
    )
    out_specs = (P("ch", VOX), P("ch", VOX), P(None, "ch", None))
    return jax.shard_map(body, mesh=split, in_specs=in_specs, out_specs=out_specs, check_vma=False)
```

```python
import math

import jax
import jax.numpy as jnp
from jax import lax
from jax.sharding import PartitionSpec as P


def owner_slots(owner_of, owners):
    labels = jnp.arange(owners, dtype=jnp.int32)
    onehot = (owner_of[:, None] == labels[None, :]).astype(jnp.int32)
    before = jnp.cumsum(onehot, axis=0) - onehot
    return jnp.sum(before * onehot, axis=1)


def one_hot(index, size):
    return (index[:, None] == jnp.arange(size, dtype=jnp.int32)[None, :]).astype(jnp.bfloat16)


def exact_sum(onehot, values):
    high = lax.reduce_precision(values, exponent_bits=8, mantissa_bits=7)
    low = values - high
    both = jnp.concatenate([high.astype(jnp.bfloat16), low.astype(jnp.bfloat16)], axis=1)
    total = jnp.einsum("pt,pc->tc", onehot, both, preferred_element_type=jnp.float32)
    width = values.shape[1]
    return total[:, :width] + total[:, width:]


VOX = ("z", "y", "core")


def flat_all_to_all(x):
    return lax.all_to_all(x, VOX, 0, 0, tiled=True)


def exact_sum_t(onehot, values):
    high = lax.reduce_precision(values, exponent_bits=8, mantissa_bits=7)
    low = values - high
    both = jnp.concatenate([high.astype(jnp.bfloat16), low.astype(jnp.bfloat16)], axis=1)
    total = jnp.einsum("pc,pt->ct", both, onehot, preferred_element_type=jnp.float32)
    width = values.shape[1]
    return total[:width] + total[width:]


def reduce_replicate(weight_sum, sizes, factor, rows):
    owners = math.prod(sizes)
    near = owners // sizes[0]
    width = weight_sum.shape[-1]
    chunk = weight_sum.size // (width * owners)
    part = weight_sum.reshape(near, sizes[0], chunk, width)
    part = lax.all_to_all(part.astype(jnp.bfloat16), VOX[1:], 0, 0, tiled=True)
    part = part.astype(jnp.float32).sum(axis=0)
    part = lax.all_to_all(part, VOX[0], 0, 0, tiled=True).sum(axis=0)
    mine = (part * factor).astype(jnp.bfloat16)
    mine = jnp.broadcast_to(mine[None], (sizes[0], chunk, width))
    mine = lax.all_to_all(mine, VOX[0], 0, 0, tiled=True)
    mine = jnp.broadcast_to(mine[None], (near, sizes[0], chunk, width))
    mine = lax.all_to_all(mine, VOX[1:], 0, 0, tiled=True)
    back = mine.reshape(owners * chunk, width)
    return back[:rows].reshape((-1,) + weight_sum.shape[1:])


def body(
    features,
    kernel,
    coarse_grad,
    pair_fine,
    pair_target,
    block_offset,
    target_owner,
    slot_coarse_row,
    fine_count,
):
    sizes = tuple(lax.axis_size(name) for name in VOX)
    owners = math.prod(sizes)
    fine_total, width_in = features.shape
    width_out, coarse_total = coarse_grad.shape
    offsets_all = kernel.shape[0]
    targets = target_owner.shape[0]
    capacity = slot_coarse_row.shape[0] // owners
    slots = owners * capacity
    blocks = block_offset.shape[0]
    pairs = pair_fine.shape[0]
    group = pairs // blocks
    live_mask = jnp.arange(fine_total, dtype=jnp.int32) < fine_count[0]
    masked = jnp.where(live_mask[:, None], features, jnp.zeros((), features.dtype))
    fine_hot = one_hot(pair_fine, fine_total)
    target_hot = one_hot(pair_target, targets)
    gathered = jnp.dot(fine_hot, masked, preferred_element_type=jnp.float32).astype(jnp.bfloat16)
    gathered = gathered.reshape(blocks, group, width_in)
    weights = kernel[block_offset]
    partial_value = jnp.einsum(
        "bpc,boc->bpo", gathered, weights, preferred_element_type=jnp.float32
    ).reshape(pairs, width_out)
    target_part = exact_sum(target_hot, partial_value).astype(jnp.bfloat16)

    owner_of = target_owner[:, 0]
    slot_index = owner_of * capacity + owner_slots(owner_of, owners)
    slot_hot = one_hot(slot_index, slots)
    send_rows = jnp.einsum(
        "ts,to->so", slot_hot, target_part, preferred_element_type=jnp.float32
    ).astype(jnp.bfloat16)
    lane_shape = (slots * width_out // 128, 128)
    received = flat_all_to_all(send_rows.reshape(lane_shape))
    got_rows = received.reshape(slots, width_out)
    row_hot = one_hot(slot_coarse_row, coarse_total)
    coarse = jnp.einsum("sc,so->co", row_hot, got_rows, preferred_element_type=jnp.float32)
    gate_output = jax.nn.sigmoid(coarse)
    activation = (coarse * gate_output).astype(jnp.bfloat16)
    grad_coarse = (
        coarse_grad.astype(jnp.float32).T * gate_output * (1.0 + coarse * (1.0 - gate_output))
    ).astype(jnp.bfloat16)
    back_rows = jnp.einsum(
        "sc,co->so", row_hot, grad_coarse, preferred_element_type=jnp.float32
    ).astype(jnp.bfloat16)
    returned = flat_all_to_all(back_rows.reshape(lane_shape))
    grad_target = jnp.einsum(
        "ts,so->to", slot_hot, returned.reshape(slots, width_out), preferred_element_type=jnp.float32
    ).astype(jnp.bfloat16)
    grad_rows = jnp.einsum(
        "pt,to->po", target_hot, grad_target, preferred_element_type=jnp.float32
    ).astype(jnp.bfloat16)
    grad_rows = grad_rows.reshape(blocks, group, width_out)
    grad_in = jnp.einsum(
        "bpo,boc->bpc", grad_rows, weights, preferred_element_type=jnp.float32
    ).reshape(pairs, width_in)
    fine_sum = exact_sum_t(fine_hot, grad_in)
    grad_weight = jnp.einsum(
        "bpc,bpo->boc", gathered, grad_rows, preferred_element_type=jnp.float32
    )
    rows_all = offsets_all * width_out
    step = owners * 8
    padded = -(-rows_all // step) * step // width_out
    offset_hot = one_hot(block_offset, padded).astype(jnp.float32)
    weight_sum = jnp.einsum(
        "bk,boc->koc", offset_hot, grad_weight, precision=lax.Precision.HIGHEST
    )
    groups = lax.axis_size("ch")
    fine_parts = fine_sum.reshape(groups, width_in // groups, fine_total)
    me = lax.axis_index("ch")
    fine_grad = lax.dynamic_index_in_dim(fine_parts, me, 0, keepdims=False)
    for shift in range(1, groups):
        outgoing = lax.dynamic_index_in_dim(fine_parts, (me + shift) % groups, 0, keepdims=False)
        pairs_of = [(i, (i + shift) % groups) for i in range(groups)]
        fine_grad = fine_grad + lax.ppermute(outgoing, "ch", pairs_of)
    grad_features = jnp.where(live_mask[None, :], fine_grad, jnp.zeros((), jnp.float32)).astype(
        jnp.bfloat16
    )
    factor = math.sqrt(offsets_all / (blocks * group * owners))
    grad_kernel = reduce_replicate(weight_sum, sizes, factor, rows_all)
    return (activation.T, grad_features, grad_kernel)


def solution(mesh):
    vox = mesh.shape["vox"]
    cores = 2
    across = 4
    split = jax.sharding.Mesh(
        mesh.devices.reshape(vox // (cores * across), across, cores, mesh.shape["ch"]),
        VOX + ("ch",),
    )
    in_specs = (
        P(VOX, None),
        P(None, "ch", None),
        P("ch", VOX),
        P(VOX),
        P(VOX),
        P(VOX),
        P(VOX, None),
        P(VOX),
        P(VOX),
    )
    out_specs = (P("ch", VOX), P("ch", VOX), P(None, "ch", None))
    return jax.shard_map(body, mesh=split, in_specs=in_specs, out_specs=out_specs, check_vma=False)
```

```python
import math

import jax
import jax.numpy as jnp
from jax import lax
from jax.sharding import PartitionSpec as P


def owner_slots(owner_of, owners):
    labels = jnp.arange(owners, dtype=jnp.int32)
    onehot = (owner_of[:, None] == labels[None, :]).astype(jnp.int32)
    before = jnp.cumsum(onehot, axis=0) - onehot
    return jnp.sum(before * onehot, axis=1)


def one_hot(index, size):
    return (index[:, None] == jnp.arange(size, dtype=jnp.int32)[None, :]).astype(jnp.bfloat16)


def exact_sum(onehot, values):
    high = lax.reduce_precision(values, exponent_bits=8, mantissa_bits=7)
    low = values - high
    both = jnp.concatenate([high.astype(jnp.bfloat16), low.astype(jnp.bfloat16)], axis=1)
    total = jnp.einsum("pt,pc->tc", onehot, both, preferred_element_type=jnp.float32)
    width = values.shape[1]
    return total[:, :width] + total[:, width:]


VOX = ("z", "y", "core")


def flat_all_to_all(x):
    return lax.all_to_all(x, VOX, 0, 0, tiled=True)


def exact_sum_t(onehot, values):
    high = lax.reduce_precision(values, exponent_bits=8, mantissa_bits=7)
    low = values - high
    both = jnp.concatenate([high.astype(jnp.bfloat16), low.astype(jnp.bfloat16)], axis=1)
    total = jnp.einsum("pc,pt->ct", both, onehot, preferred_element_type=jnp.float32)
    width = values.shape[1]
    return total[:width] + total[width:]


def reduce_replicate(weight_sum, sizes, factor, rows):
    owners = math.prod(sizes)
    near = owners // sizes[0]
    width = weight_sum.shape[-1]
    chunk = weight_sum.size // (width * owners)
    part = weight_sum.reshape(near, sizes[0], chunk, width)
    part = lax.all_to_all(part.astype(jnp.bfloat16), VOX[1:], 0, 0, tiled=True)
    part = part.astype(jnp.float32).sum(axis=0)
    part = lax.all_to_all(part, VOX[0], 0, 0, tiled=True).sum(axis=0)
    mine = (part * factor).astype(jnp.bfloat16)
    mine = jnp.broadcast_to(mine[None], (sizes[0], chunk, width))
    mine = lax.all_to_all(mine, VOX[0], 0, 0, tiled=True)
    mine = jnp.broadcast_to(mine[None], (near, sizes[0], chunk, width))
    mine = lax.all_to_all(mine, VOX[1:], 0, 0, tiled=True)
    back = mine.reshape(owners * chunk, width)
    return back[:rows].reshape((-1,) + weight_sum.shape[1:])


def body(
    features,
    kernel,
    coarse_grad,
    pair_fine,
    pair_target,
    block_offset,
    target_owner,
    slot_coarse_row,
    fine_count,
):
    sizes = tuple(lax.axis_size(name) for name in VOX)
    owners = math.prod(sizes)
    fine_total, width_in = features.shape
    width_out, coarse_total = coarse_grad.shape
    offsets_all = kernel.shape[0]
    targets = target_owner.shape[0]
    capacity = slot_coarse_row.shape[0] // owners
    slots = owners * capacity
    blocks = block_offset.shape[0]
    pairs = pair_fine.shape[0]
    group = pairs // blocks
    live_mask = jnp.arange(fine_total, dtype=jnp.int32) < fine_count[0]
    masked = jnp.where(live_mask[:, None], features, jnp.zeros((), features.dtype))
    fine_hot = one_hot(pair_fine, fine_total)
    target_hot = one_hot(pair_target, targets)
    gathered = jnp.dot(fine_hot, masked, preferred_element_type=jnp.float32).astype(jnp.bfloat16)
    gathered = gathered.reshape(blocks, group, width_in)
    weights = kernel[block_offset]
    partial_value = jnp.einsum(
        "bpc,boc->bpo", gathered, weights, preferred_element_type=jnp.float32
    ).reshape(pairs, width_out)
    target_part = exact_sum(target_hot, partial_value).astype(jnp.bfloat16)

    owner_of = target_owner[:, 0]
    slot_index = owner_of * capacity + owner_slots(owner_of, owners)
    slot_hot = one_hot(slot_index, slots)
    send_rows = jnp.einsum(
        "ts,to->so", slot_hot, target_part, preferred_element_type=jnp.float32
    ).astype(jnp.bfloat16)
    lane_shape = (slots * width_out // 128, 128)
    received = flat_all_to_all(send_rows.reshape(lane_shape))
    got_rows = received.reshape(slots, width_out)
    row_hot = one_hot(slot_coarse_row, coarse_total)
    coarse = jnp.einsum("sc,so->co", row_hot, got_rows, preferred_element_type=jnp.float32)
    gate_output = jax.nn.sigmoid(coarse)
    activation = (coarse * gate_output).astype(jnp.bfloat16)
    grad_coarse = (
        coarse_grad.astype(jnp.float32).T * gate_output * (1.0 + coarse * (1.0 - gate_output))
    ).astype(jnp.bfloat16)
    back_rows = jnp.einsum(
        "sc,co->so", row_hot, grad_coarse, preferred_element_type=jnp.float32
    ).astype(jnp.bfloat16)
    returned = flat_all_to_all(back_rows.reshape(lane_shape))
    grad_target = jnp.einsum(
        "ts,so->to", slot_hot, returned.reshape(slots, width_out), preferred_element_type=jnp.float32
    ).astype(jnp.bfloat16)
    grad_rows = jnp.einsum(
        "pt,to->po", target_hot, grad_target, preferred_element_type=jnp.float32
    ).astype(jnp.bfloat16)
    grad_rows = grad_rows.reshape(blocks, group, width_out)
    grad_in = jnp.einsum(
        "bpo,boc->bpc", grad_rows, weights, preferred_element_type=jnp.float32
    ).reshape(pairs, width_in)
    fine_sum = exact_sum_t(fine_hot, grad_in)
    grad_weight = jnp.einsum(
        "bpc,bpo->boc", gathered, grad_rows, preferred_element_type=jnp.float32
    )
    rows_all = offsets_all * width_out
    step = owners * 8
    padded = -(-rows_all // step) * step // width_out
    offset_hot = one_hot(block_offset, padded).astype(jnp.float32)
    weight_sum = jnp.einsum(
        "bk,boc->koc", offset_hot, grad_weight, precision=lax.Precision.HIGHEST
    )
    groups = lax.axis_size("ch")
    fine_parts = fine_sum.reshape(groups, width_in // groups, fine_total)
    me = lax.axis_index("ch")
    high = jnp.bitwise_and(me, 2)
    low = jnp.bitwise_and(me, 1)
    kept = lax.dynamic_slice_in_dim(fine_parts, high, 2, axis=0)
    sent = lax.dynamic_slice_in_dim(fine_parts, 2 - high, 2, axis=0)
    kept = kept + lax.ppermute(sent, "ch", [(i, i ^ 2) for i in range(groups)])
    fine_grad = lax.dynamic_index_in_dim(kept, low, 0, keepdims=False)
    sent = lax.dynamic_index_in_dim(kept, 1 - low, 0, keepdims=False)
    fine_grad = fine_grad + lax.ppermute(sent, "ch", [(i, i ^ 1) for i in range(groups)])
    grad_features = jnp.where(live_mask[None, :], fine_grad, jnp.zeros((), jnp.float32)).astype(
        jnp.bfloat16
    )
    factor = math.sqrt(offsets_all / (blocks * group * owners))
    grad_kernel = reduce_replicate(weight_sum, sizes, factor, rows_all)
    return (activation.T, grad_features, grad_kernel)


def solution(mesh):
    vox = mesh.shape["vox"]
    cores = 2
    across = 4
    split = jax.sharding.Mesh(
        mesh.devices.reshape(vox // (cores * across), across, cores, mesh.shape["ch"]),
        VOX + ("ch",),
    )
    in_specs = (
        P(VOX, None),
        P(None, "ch", None),
        P("ch", VOX),
        P(VOX),
        P(VOX),
        P(VOX),
        P(VOX, None),
        P(VOX),
        P(VOX),
    )
    out_specs = (P("ch", VOX), P("ch", VOX), P(None, "ch", None))
    return jax.shard_map(body, mesh=split, in_specs=in_specs, out_specs=out_specs, check_vma=False)
```

```python
import math

import jax
import jax.numpy as jnp
from jax import lax
from jax.sharding import PartitionSpec as P


def owner_slots(owner_of, owners):
    labels = jnp.arange(owners, dtype=jnp.int32)
    onehot = (owner_of[:, None] == labels[None, :]).astype(jnp.int32)
    before = jnp.cumsum(onehot, axis=0) - onehot
    return jnp.sum(before * onehot, axis=1)


def one_hot(index, size):
    return (index[:, None] == jnp.arange(size, dtype=jnp.int32)[None, :]).astype(jnp.bfloat16)


def exact_sum(onehot, values):
    high = lax.reduce_precision(values, exponent_bits=8, mantissa_bits=7)
    low = values - high
    both = jnp.concatenate([high.astype(jnp.bfloat16), low.astype(jnp.bfloat16)], axis=1)
    total = jnp.einsum("pt,pc->tc", onehot, both, preferred_element_type=jnp.float32)
    width = values.shape[1]
    return total[:, :width] + total[:, width:]


VOX = ("z", "y", "core")


def flat_all_to_all(x):
    return lax.all_to_all(x, VOX, 0, 0, tiled=True)


def exact_sum_t(onehot, values):
    high = lax.reduce_precision(values, exponent_bits=8, mantissa_bits=7)
    low = values - high
    both = jnp.concatenate([high.astype(jnp.bfloat16), low.astype(jnp.bfloat16)], axis=1)
    total = jnp.einsum("pc,pt->ct", both, onehot, preferred_element_type=jnp.float32)
    width = values.shape[1]
    return total[:width] + total[width:]


def reduce_replicate(weight_sum, sizes, factor, rows):
    owners = math.prod(sizes)
    near = owners // sizes[0]
    width = weight_sum.shape[-1]
    chunk = weight_sum.size // (width * owners)
    part = weight_sum.reshape(near, sizes[0], chunk, width)
    part = lax.all_to_all(part.astype(jnp.bfloat16), VOX[1:], 0, 0, tiled=True)
    part = part.astype(jnp.float32).sum(axis=0)
    part = lax.all_to_all(part, VOX[0], 0, 0, tiled=True).sum(axis=0)
    mine = (part * factor).astype(jnp.bfloat16)
    mine = jnp.broadcast_to(mine[None], (sizes[0], chunk, width))
    mine = lax.all_to_all(mine, VOX[0], 0, 0, tiled=True)
    mine = jnp.broadcast_to(mine[None], (near, sizes[0], chunk, width))
    mine = lax.all_to_all(mine, VOX[1:], 0, 0, tiled=True)
    back = mine.reshape(owners * chunk, width)
    return back[:rows].reshape((-1,) + weight_sum.shape[1:])


def body(
    features,
    kernel,
    coarse_grad,
    pair_fine,
    pair_target,
    block_offset,
    target_owner,
    slot_coarse_row,
    fine_count,
):
    sizes = tuple(lax.axis_size(name) for name in VOX)
    owners = math.prod(sizes)
    fine_total, width_in = features.shape
    width_out, coarse_total = coarse_grad.shape
    offsets_all = kernel.shape[0]
    targets = target_owner.shape[0]
    capacity = slot_coarse_row.shape[0] // owners
    slots = owners * capacity
    blocks = block_offset.shape[0]
    pairs = pair_fine.shape[0]
    group = pairs // blocks
    live_mask = jnp.arange(fine_total, dtype=jnp.int32) < fine_count[0]
    masked = jnp.where(live_mask[:, None], features, jnp.zeros((), features.dtype))
    fine_hot = one_hot(pair_fine, fine_total)
    target_hot = one_hot(pair_target, targets)
    gathered = jnp.dot(fine_hot, masked, preferred_element_type=jnp.float32).astype(jnp.bfloat16)
    gathered = gathered.reshape(blocks, group, width_in)
    weights = kernel[block_offset]
    partial_value = jnp.einsum(
        "bpc,boc->bpo", gathered, weights, preferred_element_type=jnp.float32
    ).reshape(pairs, width_out)
    target_part = exact_sum(target_hot, partial_value).astype(jnp.bfloat16)

    owner_of = target_owner[:, 0]
    slot_index = owner_of * capacity + owner_slots(owner_of, owners)
    slot_hot = one_hot(slot_index, slots)
    send_rows = jnp.einsum(
        "ts,to->so", slot_hot, target_part, preferred_element_type=jnp.float32
    ).astype(jnp.bfloat16)
    lane_shape = (slots * width_out // 128, 128)
    received = flat_all_to_all(send_rows.reshape(lane_shape))
    got_rows = received.reshape(slots, width_out)
    row_hot = one_hot(slot_coarse_row, coarse_total)
    coarse = jnp.einsum("sc,so->co", row_hot, got_rows, preferred_element_type=jnp.float32)
    gate_output = jax.nn.sigmoid(coarse)
    activation = (coarse * gate_output).astype(jnp.bfloat16)
    grad_coarse = (
        coarse_grad.astype(jnp.float32).T * gate_output * (1.0 + coarse * (1.0 - gate_output))
    ).astype(jnp.bfloat16)
    back_rows = jnp.einsum(
        "sc,co->so", row_hot, grad_coarse, preferred_element_type=jnp.float32
    ).astype(jnp.bfloat16)
    returned = flat_all_to_all(back_rows.reshape(lane_shape))
    grad_target = jnp.einsum(
        "ts,so->to", slot_hot, returned.reshape(slots, width_out), preferred_element_type=jnp.float32
    ).astype(jnp.bfloat16)
    grad_rows = jnp.einsum(
        "pt,to->po", target_hot, grad_target, preferred_element_type=jnp.float32
    ).astype(jnp.bfloat16)
    grad_rows = grad_rows.reshape(blocks, group, width_out)
    grad_in = jnp.einsum(
        "bpo,boc->bpc", grad_rows, weights, preferred_element_type=jnp.float32
    ).reshape(pairs, width_in)
    fine_sum = exact_sum_t(fine_hot, grad_in)
    grad_weight = jnp.einsum(
        "bpc,bpo->boc", gathered, grad_rows, preferred_element_type=jnp.float32
    )
    rows_all = offsets_all * width_out
    step = owners * 8
    padded = -(-rows_all // step) * step // width_out
    offset_hot = (
        jnp.arange(padded, dtype=jnp.int32)[:, None] == block_offset[None, :]
    ).astype(jnp.float32)
    weight_sum = jnp.dot(
        offset_hot, grad_weight.reshape(blocks, -1), precision=lax.Precision.HIGHEST
    ).reshape(padded, width_out, width_in)
    groups = lax.axis_size("ch")
    fine_parts = fine_sum.reshape(groups, width_in // groups, fine_total)
    me = lax.axis_index("ch")
    high = jnp.bitwise_and(me, 2)
    low = jnp.bitwise_and(me, 1)
    kept = lax.dynamic_slice_in_dim(fine_parts, high, 2, axis=0)
    sent = lax.dynamic_slice_in_dim(fine_parts, 2 - high, 2, axis=0)
    kept = kept + lax.ppermute(sent, "ch", [(i, i ^ 2) for i in range(groups)])
    fine_grad = lax.dynamic_index_in_dim(kept, low, 0, keepdims=False)
    sent = lax.dynamic_index_in_dim(kept, 1 - low, 0, keepdims=False)
    fine_grad = fine_grad + lax.ppermute(sent, "ch", [(i, i ^ 1) for i in range(groups)])
    grad_features = jnp.where(live_mask[None, :], fine_grad, jnp.zeros((), jnp.float32)).astype(
        jnp.bfloat16
    )
    factor = math.sqrt(offsets_all / (blocks * group * owners))
    grad_kernel = reduce_replicate(weight_sum, sizes, factor, rows_all)
    return (activation.T, grad_features, grad_kernel)


def solution(mesh):
    vox = mesh.shape["vox"]
    cores = 2
    across = 4
    split = jax.sharding.Mesh(
        mesh.devices.reshape(vox // (cores * across), across, cores, mesh.shape["ch"]),
        VOX + ("ch",),
    )
    in_specs = (
        P(VOX, None),
        P(None, "ch", None),
        P("ch", VOX),
        P(VOX),
        P(VOX),
        P(VOX),
        P(VOX, None),
        P(VOX),
        P(VOX),
    )
    out_specs = (P("ch", VOX), P("ch", VOX), P(None, "ch", None))
    return jax.shard_map(body, mesh=split, in_specs=in_specs, out_specs=out_specs, check_vma=False)
```

```python
import math

import jax
import jax.numpy as jnp
from jax import lax
from jax.sharding import PartitionSpec as P


def owner_slots(owner_of, owners):
    labels = jnp.arange(owners, dtype=jnp.int32)
    onehot = (owner_of[:, None] == labels[None, :]).astype(jnp.bfloat16)
    rows = jnp.arange(owner_of.shape[0], dtype=jnp.int32)
    earlier = (rows[None, :] < rows[:, None]).astype(jnp.bfloat16)
    before = jnp.dot(earlier, onehot, preferred_element_type=jnp.float32)
    return jnp.sum(before * onehot.astype(jnp.float32), axis=1).astype(jnp.int32)


def one_hot(index, size):
    return (index[:, None] == jnp.arange(size, dtype=jnp.int32)[None, :]).astype(jnp.bfloat16)


def exact_sum(onehot, values):
    high = lax.reduce_precision(values, exponent_bits=8, mantissa_bits=7)
    low = values - high
    both = jnp.concatenate([high.astype(jnp.bfloat16), low.astype(jnp.bfloat16)], axis=1)
    total = jnp.einsum("pt,pc->tc", onehot, both, preferred_element_type=jnp.float32)
    width = values.shape[1]
    return total[:, :width] + total[:, width:]


VOX = ("z", "y", "core")


def flat_all_to_all(x):
    return lax.all_to_all(x, VOX, 0, 0, tiled=True)


def exact_sum_t(onehot, values):
    high = lax.reduce_precision(values, exponent_bits=8, mantissa_bits=7)
    low = values - high
    both = jnp.concatenate([high.astype(jnp.bfloat16), low.astype(jnp.bfloat16)], axis=1)
    total = jnp.einsum("pc,pt->ct", both, onehot, preferred_element_type=jnp.float32)
    width = values.shape[1]
    return total[:width] + total[width:]


def reduce_replicate(weight_sum, sizes, factor, rows):
    owners = math.prod(sizes)
    near = owners // sizes[0]
    width = weight_sum.shape[-1]
    chunk = weight_sum.size // (width * owners)
    part = weight_sum.reshape(near, sizes[0], chunk, width)
    part = lax.all_to_all(part.astype(jnp.bfloat16), VOX[1:], 0, 0, tiled=True)
    part = part.astype(jnp.float32).sum(axis=0)
    part = lax.all_to_all(part, VOX[0], 0, 0, tiled=True).sum(axis=0)
    mine = (part * factor).astype(jnp.bfloat16)
    mine = jnp.broadcast_to(mine[None], (sizes[0], chunk, width))
    mine = lax.all_to_all(mine, VOX[0], 0, 0, tiled=True)
    mine = jnp.broadcast_to(mine[None], (near, sizes[0], chunk, width))
    mine = lax.all_to_all(mine, VOX[1:], 0, 0, tiled=True)
    back = mine.reshape(owners * chunk, width)
    return back[:rows].reshape((-1,) + weight_sum.shape[1:])


def body(
    features,
    kernel,
    coarse_grad,
    pair_fine,
    pair_target,
    block_offset,
    target_owner,
    slot_coarse_row,
    fine_count,
):
    sizes = tuple(lax.axis_size(name) for name in VOX)
    owners = math.prod(sizes)
    fine_total, width_in = features.shape
    width_out, coarse_total = coarse_grad.shape
    offsets_all = kernel.shape[0]
    targets = target_owner.shape[0]
    capacity = slot_coarse_row.shape[0] // owners
    slots = owners * capacity
    blocks = block_offset.shape[0]
    pairs = pair_fine.shape[0]
    group = pairs // blocks
    live_mask = jnp.arange(fine_total, dtype=jnp.int32) < fine_count[0]
    masked = jnp.where(live_mask[:, None], features, jnp.zeros((), features.dtype))
    fine_hot = one_hot(pair_fine, fine_total)
    target_hot = one_hot(pair_target, targets)
    gathered = jnp.dot(fine_hot, masked, preferred_element_type=jnp.float32).astype(jnp.bfloat16)
    gathered = gathered.reshape(blocks, group, width_in)
    weights = kernel[block_offset]
    partial_value = jnp.einsum(
        "bpc,boc->bpo", gathered, weights, preferred_element_type=jnp.float32
    ).reshape(pairs, width_out)
    target_part = exact_sum(target_hot, partial_value).astype(jnp.bfloat16)

    owner_of = target_owner[:, 0]
    slot_index = owner_of * capacity + owner_slots(owner_of, owners)
    slot_hot = one_hot(slot_index, slots)
    send_rows = jnp.einsum(
        "ts,to->so", slot_hot, target_part, preferred_element_type=jnp.float32
    ).astype(jnp.bfloat16)
    lane_shape = (slots * width_out // 128, 128)
    received = flat_all_to_all(send_rows.reshape(lane_shape))
    got_rows = received.reshape(slots, width_out)
    row_hot = one_hot(slot_coarse_row, coarse_total)
    coarse = jnp.einsum("sc,so->co", row_hot, got_rows, preferred_element_type=jnp.float32)
    gate_output = jax.nn.sigmoid(coarse)
    activation = (coarse * gate_output).astype(jnp.bfloat16)
    grad_coarse = (
        coarse_grad.astype(jnp.float32).T * gate_output * (1.0 + coarse * (1.0 - gate_output))
    ).astype(jnp.bfloat16)
    back_rows = jnp.einsum(
        "sc,co->so", row_hot, grad_coarse, preferred_element_type=jnp.float32
    ).astype(jnp.bfloat16)
    returned = flat_all_to_all(back_rows.reshape(lane_shape))
    grad_target = jnp.einsum(
        "ts,so->to", slot_hot, returned.reshape(slots, width_out), preferred_element_type=jnp.float32
    ).astype(jnp.bfloat16)
    grad_rows = jnp.einsum(
        "pt,to->po", target_hot, grad_target, preferred_element_type=jnp.float32
    ).astype(jnp.bfloat16)
    grad_rows = grad_rows.reshape(blocks, group, width_out)
    grad_in = jnp.einsum(
        "bpo,boc->bpc", grad_rows, weights, preferred_element_type=jnp.float32
    ).reshape(pairs, width_in)
    fine_sum = exact_sum_t(fine_hot, grad_in)
    grad_weight = jnp.einsum(
        "bpc,bpo->boc", gathered, grad_rows, preferred_element_type=jnp.float32
    )
    rows_all = offsets_all * width_out
    step = owners * 8
    padded = -(-rows_all // step) * step // width_out
    offset_hot = (
        jnp.arange(padded, dtype=jnp.int32)[:, None] == block_offset[None, :]
    ).astype(jnp.float32)
    weight_sum = jnp.dot(
        offset_hot, grad_weight.reshape(blocks, -1), precision=lax.Precision.HIGHEST
    ).reshape(padded, width_out, width_in)
    groups = lax.axis_size("ch")
    fine_parts = fine_sum.reshape(groups, width_in // groups, fine_total)
    me = lax.axis_index("ch")
    high = jnp.bitwise_and(me, 2)
    low = jnp.bitwise_and(me, 1)
    kept = lax.dynamic_slice_in_dim(fine_parts, high, 2, axis=0)
    sent = lax.dynamic_slice_in_dim(fine_parts, 2 - high, 2, axis=0)
    kept = kept + lax.ppermute(sent, "ch", [(i, i ^ 2) for i in range(groups)])
    fine_grad = lax.dynamic_index_in_dim(kept, low, 0, keepdims=False)
    sent = lax.dynamic_index_in_dim(kept, 1 - low, 0, keepdims=False)
    fine_grad = fine_grad + lax.ppermute(sent, "ch", [(i, i ^ 1) for i in range(groups)])
    grad_features = jnp.where(live_mask[None, :], fine_grad, jnp.zeros((), jnp.float32)).astype(
        jnp.bfloat16
    )
    factor = math.sqrt(offsets_all / (blocks * group * owners))
    grad_kernel = reduce_replicate(weight_sum, sizes, factor, rows_all)
    return (activation.T, grad_features, grad_kernel)


def solution(mesh):
    vox = mesh.shape["vox"]
    cores = 2
    across = 4
    split = jax.sharding.Mesh(
        mesh.devices.reshape(vox // (cores * across), across, cores, mesh.shape["ch"]),
        VOX + ("ch",),
    )
    in_specs = (
        P(VOX, None),
        P(None, "ch", None),
        P("ch", VOX),
        P(VOX),
        P(VOX),
        P(VOX),
        P(VOX, None),
        P(VOX),
        P(VOX),
    )
    out_specs = (P("ch", VOX), P("ch", VOX), P(None, "ch", None))
    return jax.shard_map(body, mesh=split, in_specs=in_specs, out_specs=out_specs, check_vma=False)
```
